256 devices in a mesh: seq: 32 (over z, y), tp: 8 (over x, core).
Axes of the slice: x: 4, y: 4, z: 8, core: 2. Of those that a mesh axis runs over, the one named last changes fastest.
Arguments:
- tokens: bfloat16 [384, 4096], P(None, 'seq'), may hold values from -30 to 30
- ln_first_gain: bfloat16 [4096], P('seq'), may hold values from 0.099609375 to 1.8984375
- w_qkv: bfloat16 [4096, 3, 4096], P('seq', None, 'tp'), may hold values from -0.25 to 0.25
- w_out: bfloat16 [4096, 4096], P('tp', 'seq'), may hold values from -1 to 1
- ln_second_gain: bfloat16 [4096], P('seq'), may hold values from 0.099609375 to 1.8984375
- w_up: bfloat16 [4096, 16384], P('seq', 'tp'), may hold values from -0.09375 to 0.09375
- w_down: bfloat16 [16384, 4096], P('tp', 'seq'), may hold values from -0.09375 to 0.09375
- prompt_key: bfloat16 [8, 16384, 4096], P(None, 'seq', 'tp'), may hold values from -200 to 200
- prompt_val: bfloat16 [8, 16384, 4096], P(None, 'seq', 'tp'), may hold values from -20 to 20
- cont_key: bfloat16 [96, 256, 4096], P('seq', None, 'tp'), may hold values from -18 to 18
- cont_val: bfloat16 [96, 256, 4096], P('seq', None, 'tp'), may hold values from -20 to 20
- group_ids: int32 [96], replicated, may hold values from 0 to 7, as said below
- prompt_len: int32 [8], replicated, may hold values from 1 to 16384, as said below
- cont_len: int32 [96], replicated, may hold values from 0 to 252, as said below
Outputs:
- layer_out: bfloat16 [384, 4096], P(None, 'seq')
The draws below stay inside these ranges and needn't reach their ends.
Inputs may be any that keep to these rules, and one draw needn't show every extreme that they name: `group_ids`: each of the 8 groups is named by exactly 12 requests. `prompt_len`: one group's prompt has exactly 16384 positions. `cont_len`: some request has exactly 252 filled slots.
All inputs are finite; a program needn't handle non-finite values.
Results may differ from the reference program's by a relative error of at most 0.013.
The reference program's roundings to bfloat16 on the way count: a program that leaves them out, or rounds other values in their place, can miss the bound.
Values may be sent and summed in bfloat16 or wider, within the bound.
No kernel may reach another device: no remote copies, remote signals or barrier semaphores. Data moves between devices by JAX's collectives and lax.ppermute only.
A program may use at most 128 MiB of HBM per device.

```python
import math
import jax
import jax.numpy as jnp
from jax import lax

D = 4096
HEADS = 32
HD = 128
FF = 16384
NEW = 4
GROUP_REQ = 12
CONT = 256
PROMPT_DEV = 512
REQS = 96
GROUPS = 8
ROWS = 384
PROMPT = 16384
N_SEQ = 32


def feature_signs(key):
    return jax.random.rademacher(jax.random.fold_in(key, 101), (D,), jnp.float32)


def value_noise(key, shape):
    noise = 3.0 * jnp.clip(jax.random.normal(key, shape, jnp.float32), -6.0, 6.0)
    return noise


def draw_tokens(key, part):
    subkeys = jax.random.split(key, 3)
    row_scale = jnp.exp(jax.random.uniform(subkeys[1], (ROWS, 1), jnp.float32, math.log(0.5), math.log(2.0)))
    col_ramp = jnp.power(3.0, jnp.arange(D, dtype=jnp.float32) / D)[None, :]
    col_scale = 0.7 * col_ramp * jnp.exp(jax.random.uniform(subkeys[2], (1, D), jnp.float32, math.log(0.7), math.log(1.4)))
    normal_part = jnp.clip(jax.random.normal(subkeys[0], (ROWS, D), jnp.float32), -4.0, 4.0)
    result = row_scale * col_scale * normal_part
    return result.astype(jnp.bfloat16)


def draw_w_out(key, part):
    subkeys = jax.random.split(jax.random.fold_in(key, 202), 2)
    signs = feature_signs(key)
    base = jnp.clip(jax.random.normal(subkeys[0], (D, D), jnp.float32), -4.0, 4.0) / math.sqrt(D)
    column_part = jnp.clip(jax.random.normal(subkeys[1], (D,), jnp.float32), -4.0, 4.0)
    result = base + 4.0 / (3.0 * D) * signs[:, None] * column_part[None, :]
    return result.astype(jnp.bfloat16)


def draw_prompt_val(key, part):
    signs = feature_signs(key)
    noise = value_noise(jax.random.fold_in(key, 303), (GROUPS, PROMPT, D))
    return (noise + 1.5 * signs[None, None, :]).astype(jnp.bfloat16)


def draw_cont_val(key, part):
    signs = feature_signs(key)
    noise = value_noise(jax.random.fold_in(key, 404), (REQS, CONT, D))
    return (noise + 1.5 * signs[None, None, :]).astype(jnp.bfloat16)


def draw_prompt_key(key, part):
    subkeys = jax.random.split(key, 1)
    result = 3.0 * jnp.clip(jax.random.normal(subkeys[0], (GROUPS, PROMPT, D), jnp.float32), -6.0, 6.0)
    return result.astype(jnp.bfloat16)


def draw_group_ids(key, part):
    order = jax.random.permutation(key, REQS)
    return (order % GROUPS).astype(jnp.int32)


def draw_prompt_len(key, part):
    lengths = jax.random.randint(key, (GROUPS,), 1, PROMPT + 1)
    longest = jax.random.randint(jax.random.fold_in(key, 7), (), 0, GROUPS)
    return jnp.where(jnp.arange(GROUPS) == longest, PROMPT, lengths).astype(jnp.int32)


def draw_cont_len(key, part):
    lengths = jax.random.randint(key, (REQS,), 0, CONT - NEW + 1)
    longest = jax.random.randint(jax.random.fold_in(key, 11), (), 0, REQS)
    return jnp.where(jnp.arange(REQS) == longest, CONT - NEW, lengths).astype(jnp.int32)


def block_levels(key, extent, cuts, smallest, largest):
    loudness, own = 1.0, jax.random.fold_in(key, 6)
    for dim, shards_of in cuts:
        steps = jnp.exp(jax.random.uniform(jax.random.fold_in(own, dim), (shards_of,), jnp.float32, smallest / len(cuts), largest / len(cuts)))
        loudness = loudness * jnp.repeat(steps, extent[dim] // shards_of).reshape([-1 if axis == dim else 1 for axis in range(len(extent))])
    return loudness


def normal_values(rng, extent, deviation, reach, cuts=(), kind=jnp.bfloat16):
    values = jax.random.normal(rng, extent, jnp.float32) * deviation
    if len(cuts) > 0:
        values = block_levels(rng, extent, cuts, -0.22, 0.18) * values
    return jnp.clip(values, min=-reach, max=reach).astype(kind)


def setup_inputs(seed: int = 0) -> dict:
    key_list = jax.random.split(jax.random.key(seed), 15)
    return {
        "tokens": draw_tokens(jax.random.fold_in(key_list[14], 71), 0),
        "ln_first_gain": jnp.clip(1.0 + 0.18 * jax.random.normal(key_list[1], (D,), jnp.float32), 0.099609375, 1.8984375).astype(jnp.bfloat16),
        "w_qkv": normal_values(key_list[2], (D, 3, D), (D // 9) ** -0.5, 0.25, ((0, 32), (2, 8))),
        "w_out": draw_w_out(jax.random.fold_in(key_list[14], 71), 0),
        "ln_second_gain": jnp.clip(1.0 + 0.18 * jax.random.normal(key_list[4], (D,), jnp.float32), 0.099609375, 1.8984375).astype(jnp.bfloat16),
        "w_up": normal_values(key_list[5], (D, FF), D ** -0.5, 0.09375, ((0, 32), (1, 8))),
        "w_down": normal_values(key_list[6], (FF, D), (FF // 4) ** -0.5, 0.09375, ((0, 8), (1, 32))),
        "prompt_key": draw_prompt_key(jax.random.fold_in(key_list[14], 71), 0),
        "prompt_val": draw_prompt_val(jax.random.fold_in(key_list[14], 71), 0),
        "cont_key": normal_values(key_list[9], (REQS, CONT, D), 3.0, 18.0, ((0, 32), (2, 8))),
        "cont_val": draw_cont_val(jax.random.fold_in(key_list[14], 71), 0),
        "group_ids": draw_group_ids(jax.random.fold_in(key_list[14], 71), 0),
        "prompt_len": draw_prompt_len(jax.random.fold_in(key_list[14], 71), 0),
        "cont_len": draw_cont_len(jax.random.fold_in(key_list[14], 71), 0),
    }


NEG_FILL = -1e+30
NORM_EPS = 1e-05

def layer_norm(values, gain):
    mean_row = lax.optimization_barrier(jnp.sum(values, 1)) / D
    variance = lax.optimization_barrier(jnp.sum(values * values, 1)) / D - mean_row * mean_row
    scaled = (values - mean_row[:, None]) * lax.rsqrt(variance + NORM_EPS)[:, None]
    return (scaled * gain.astype(jnp.float32)[None, :]).astype(jnp.bfloat16)

def reference(tokens, ln_first_gain, w_qkv, w_out, ln_second_gain, w_up, w_down, prompt_key, prompt_val, cont_key, cont_val, group_ids, prompt_len, cont_len):
    token_float = tokens.astype(jnp.float32)
    normed = layer_norm(token_float, ln_first_gain)
    projected = jnp.dot(normed, w_qkv.reshape(D, 3 * D), preferred_element_type=jnp.float32).astype(jnp.bfloat16)
    query = projected[:, :D]
    key_new = projected[:, D:2 * D]
    val_new = projected[:, 2 * D:]
    score_scale = 1.0 / math.sqrt(HD)
    slopes = jnp.exp2(-8.0 * (jnp.arange(HEADS, dtype=jnp.float32) + 1.0) / HEADS)
    members = jnp.argsort(group_ids, stable=True).astype(jnp.int32).reshape(GROUPS, GROUP_REQ)
    inverse = jnp.argsort(members.reshape(-1)).astype(jnp.int32)
    req_prompt = prompt_len[group_ids]
    query_pos = (req_prompt + cont_len)[:, None] + jnp.arange(NEW, dtype=jnp.int32)[None, :]
    query_req = query.astype(jnp.float32).reshape(REQS, NEW, HEADS, HD)

    def one_group(group_item):
        group_keys, group_vals, chosen, length = group_item
        group_query = query_req[chosen].reshape(GROUP_REQ * NEW, HEADS, HD)
        group_pos = query_pos[chosen].reshape(GROUP_REQ * NEW)
        key_blocks = group_keys.astype(jnp.float32).reshape(N_SEQ, PROMPT_DEV, HEADS, HD)
        val_blocks = group_vals.astype(jnp.float32).reshape(N_SEQ, PROMPT_DEV, HEADS, HD)
        scores = jnp.einsum('qhd,bphd->bhqp', group_query, key_blocks)
        key_pos = jnp.arange(PROMPT, dtype=jnp.int32).reshape(N_SEQ, PROMPT_DEV)
        distance = (key_pos[:, None, :] - group_pos[None, :, None]).astype(jnp.float32)
        scores = scores * score_scale + slopes[None, :, None, None] * distance[:, None, :, :]
        is_live = (key_pos < length)[:, None, None, :]
        block_top = lax.optimization_barrier(jnp.max(jnp.where(is_live, scores, NEG_FILL), -1))
        weights = jnp.where(is_live, jnp.exp(scores - block_top[..., None]), 0.0)
        block_sum = lax.optimization_barrier(jnp.sum(weights, -1))
        block_acc = jnp.einsum('bhqp,bphd->bqhd', weights.astype(jnp.bfloat16).astype(jnp.float32), val_blocks)
        group_top = lax.optimization_barrier(jnp.max(block_top, 0))
        factor = jnp.exp(block_top - group_top[None])
        group_sum = lax.optimization_barrier(jnp.sum(factor * block_sum, 0))
        group_acc = jnp.einsum('bhq,bqhd->qhd', factor, block_acc)
        return (group_top.T, group_sum.T, group_acc)
    tops, sums, accs = lax.map(one_group, (prompt_key, prompt_val, members, prompt_len))
    prompt_top = tops.reshape(REQS, NEW, HEADS)[inverse]
    prompt_sum = sums.reshape(REQS, NEW, HEADS)[inverse]
    prompt_acc = accs.reshape(REQS, NEW, HEADS, HD)[inverse]
    cache_keys = cont_key.astype(jnp.float32).reshape(REQS, CONT, HEADS, HD)
    cache_vals = cont_val.astype(jnp.float32).reshape(REQS, CONT, HEADS, HD)
    cache_pos = req_prompt[:, None] + jnp.arange(CONT, dtype=jnp.int32)[None, :]
    cache_scores = jnp.einsum('rjhd,rkhd->rhjk', query_req, cache_keys) * score_scale
    cache_scores = cache_scores + slopes[None, :, None, None] * (cache_pos[:, None, None, :] - query_pos[:, None, :, None]).astype(jnp.float32)
    cache_live = (jnp.arange(CONT, dtype=jnp.int32)[None, :] < cont_len[:, None])[:, None, None, :]
    fresh_keys = key_new.astype(jnp.float32).reshape(REQS, NEW, HEADS, HD)
    fresh_vals = val_new.astype(jnp.float32).reshape(REQS, NEW, HEADS, HD)
    steps_new = jnp.arange(NEW, dtype=jnp.int32)
    fresh_dist = (steps_new[None, :] - steps_new[:, None]).astype(jnp.float32)
    fresh_scores = jnp.einsum('rjhd,rkhd->rhjk', query_req, fresh_keys) * score_scale
    fresh_scores = fresh_scores + slopes[None, :, None, None] * fresh_dist[None, None, :, :]
    fresh_live = (steps_new[None, :] <= steps_new[:, None])[None, None, :, :]
    home_top = jnp.maximum(lax.optimization_barrier(jnp.max(jnp.where(cache_live, cache_scores, NEG_FILL), -1)), lax.optimization_barrier(jnp.max(jnp.where(fresh_live, fresh_scores, NEG_FILL), -1)))
    cache_weights = jnp.where(cache_live, jnp.exp(cache_scores - home_top[..., None]), 0.0)
    fresh_weights = jnp.where(fresh_live, jnp.exp(fresh_scores - home_top[..., None]), 0.0)
    home_sum = lax.optimization_barrier(jnp.sum(cache_weights, -1)) + lax.optimization_barrier(jnp.sum(fresh_weights, -1))
    home_acc = jnp.einsum('rhjk,rkhd->rjhd', cache_weights.astype(jnp.bfloat16).astype(jnp.float32), cache_vals)
    home_acc = home_acc + jnp.einsum('rhjk,rkhd->rjhd', fresh_weights.astype(jnp.bfloat16).astype(jnp.float32), fresh_vals)
    home_top = jnp.transpose(home_top, (0, 2, 1))
    home_sum = jnp.transpose(home_sum, (0, 2, 1))
    merged_top = jnp.maximum(prompt_top, home_top)
    left_factor = jnp.exp(prompt_top - merged_top)
    right_factor = jnp.exp(home_top - merged_top)
    denom = prompt_sum * left_factor + home_sum * right_factor
    numer = prompt_acc * left_factor[..., None] + home_acc * right_factor[..., None]
    attended = (numer / denom[..., None]).reshape(ROWS, D).astype(jnp.bfloat16)
    hidden_state = token_float + jnp.dot(attended, w_out, preferred_element_type=jnp.float32)
    second_normed = layer_norm(hidden_state, ln_second_gain)
    up_sum = jnp.dot(second_normed, w_up, preferred_element_type=jnp.float32)
    activated = jax.nn.gelu(up_sum, approximate=False).astype(jnp.bfloat16)
    down_sum = jnp.dot(activated, w_down, preferred_element_type=jnp.float32)
    return (hidden_state + down_sum).astype(jnp.bfloat16)
```

```python
import math

import jax
import jax.numpy as jnp
from jax import lax
from jax.sharding import PartitionSpec as P

D = 4096
HEADS = 32
HD = 128
NEW = 4


NEG_FILL = -1e30
NORM_EPS = 1e-05


def finish_norm(values, row_sum, row_square, gain):
    mean_row = row_sum / D
    variance = row_square / D - mean_row * mean_row
    scaled = (values - mean_row[:, None]) * lax.rsqrt(variance + NORM_EPS)[:, None]
    return (scaled * gain.astype(jnp.float32)[None, :]).astype(jnp.bfloat16)


def combine_parts(earlier, later):
    merged_top = jnp.maximum(earlier[0], later[0])
    left_factor = jnp.exp(earlier[0] - merged_top)
    right_factor = jnp.exp(later[0] - merged_top)
    merged_sum = earlier[1] * left_factor + later[1] * right_factor
    merged_acc = earlier[2] * left_factor[..., None] + later[2] * right_factor[..., None]
    return (merged_top, merged_sum, merged_acc)


def _levels(n):
    return n.bit_length() - 1


def _pairs(n, bit):
    return [(i, i ^ (1 << bit)) for i in range(n)]


def ar_doubling(x, axis, n, order):
    for bit in order:
        x = x + lax.ppermute(x, axis, _pairs(n, bit))
    return x


def add_parts(keep, got):
    return tuple(a + b for a, b in zip(keep, got))


def rs_halving(parts, axis, n, order, index, merge):
    levels = _levels(n)
    parts = tuple(p.reshape((2,) * levels + (p.shape[0] // n,) + p.shape[1:]) for p in parts)
    remaining = list(range(levels - 1, -1, -1))
    for bit in order:
        ax = remaining.index(bit)
        mine = (index >> bit) & 1
        keep = tuple(lax.dynamic_index_in_dim(p, mine, ax, keepdims=False) for p in parts)
        send = tuple(lax.dynamic_index_in_dim(p, 1 - mine, ax, keepdims=False) for p in parts)
        got = lax.ppermute(send, axis, _pairs(n, bit))
        parts = merge(keep, got)
        remaining.remove(bit)
    return parts


def ag_doubling(x, axis, n, order, index):
    levels = _levels(n)
    have = []
    for bit in order:
        got = lax.ppermute(x, axis, _pairs(n, bit))
        first = ((index >> bit) & 1) == 0
        low = jnp.where(first, x, got)
        high = jnp.where(first, got, x)
        pos = sum(1 for b in have if b > bit)
        x = jnp.stack([low, high], axis=pos)
        have.insert(pos, bit)
    return x.reshape((-1,) + x.shape[levels + 1 :])


def seq_orders(n):
    levels = _levels(n)
    near = [b for b in (0, 2, 1, 3, 4) if b < levels] + list(range(5, levels))
    return near, near[::-1]


def tp_order(n):
    return list(range(_levels(n)))


def body(
    tokens,
    ln_first_gain,
    w_qkv,
    w_out,
    ln_second_gain,
    w_up,
    w_down,
    prompt_key,
    prompt_val,
    cont_key,
    cont_val,
    group_ids,
    prompt_len,
    cont_len,
):
    row_count = tokens.shape[0]
    seq_index = lax.axis_index("seq")
    tp_index = lax.axis_index("tp")
    n_seq = lax.axis_size("seq")
    n_tp = lax.axis_size("tp")
    halve_order, double_order = seq_orders(n_seq)
    tp_bits = tp_order(n_tp)
    feat_width = w_qkv.shape[2]
    local_heads = feat_width // HD
    home_requests = cont_key.shape[0]
    home_rows = home_requests * NEW
    requests = row_count // NEW
    groups = prompt_key.shape[0]
    block_len = prompt_key.shape[1]
    slots = cont_key.shape[1]
    score_scale = 1.0 / math.sqrt(HD)
    token_float = tokens.astype(jnp.float32)
    first_stats = ar_doubling(
        jnp.stack([jnp.sum(token_float, 1), jnp.sum(token_float * token_float, 1)]),
        "seq", n_seq, halve_order,
    )
    normed = finish_norm(token_float, first_stats[0], first_stats[1], ln_first_gain)
    w_flat = w_qkv.reshape(w_qkv.shape[0], 3 * feat_width)
    partial_qkv = jnp.dot(normed, w_flat, preferred_element_type=jnp.float32)
    (own_qkv,) = rs_halving((partial_qkv,), "seq", n_seq, halve_order, seq_index, add_parts)
    own_qkv = own_qkv.astype(jnp.bfloat16)
    query = ag_doubling(own_qkv[:, :feat_width], "seq", n_seq, double_order, seq_index)
    key_new = own_qkv[:, feat_width : 2 * feat_width]
    val_new = own_qkv[:, 2 * feat_width :]
    head_first = (tp_index * local_heads).astype(jnp.float32)
    slopes = jnp.exp2(
        -8.0 * (head_first + jnp.arange(local_heads, dtype=jnp.float32) + 1.0) / HEADS
    )
    members = jnp.argsort(group_ids, stable=True).reshape(groups, requests // groups)
    inverse = jnp.argsort(members.reshape(-1))
    group_match = group_ids[:, None] == jnp.arange(groups, dtype=jnp.int32)[None, :]
    req_prompt = jnp.sum(jnp.where(group_match, prompt_len[None, :], 0), 1)
    query_pos = (req_prompt + cont_len)[:, None] + jnp.arange(NEW, dtype=jnp.int32)[None, :]
    query_req = query.reshape(requests, NEW, local_heads, HD)
    group_query = query_req[members].reshape(groups, -1, local_heads, HD)
    group_pos = query_pos[members].reshape(groups, -1)
    key_slab = prompt_key.reshape(groups, block_len, local_heads, HD)
    val_slab = prompt_val.reshape(groups, block_len, local_heads, HD)
    key_pos = seq_index * block_len + jnp.arange(block_len, dtype=jnp.int32)
    scores = jnp.einsum(
        "gqhd,gphd->ghqp", group_query, key_slab, preferred_element_type=jnp.float32
    )
    distance = (key_pos[None, None, :] - group_pos[:, :, None]).astype(jnp.float32)
    scores = scores * score_scale + slopes[None, :, None, None] * distance[:, None, :, :]
    is_live = (key_pos[None, :] < prompt_len[:, None])[:, None, None, :]
    block_top = jnp.max(jnp.where(is_live, scores, NEG_FILL), -1)
    weights = jnp.where(is_live, jnp.exp(scores - block_top[..., None]), 0.0)
    block_sum = jnp.sum(weights, -1)
    block_acc = jnp.einsum(
        "ghqp,gphd->gqhd",
        weights.astype(jnp.bfloat16),
        val_slab,
        preferred_element_type=jnp.float32,
    )
    prompt_top = (
        jnp.transpose(block_top, (0, 2, 1))
        .reshape(requests, NEW, local_heads)[inverse]
        .reshape(row_count, local_heads)
    )
    prompt_sum = (
        jnp.transpose(block_sum, (0, 2, 1))
        .reshape(requests, NEW, local_heads)[inverse]
        .reshape(row_count, local_heads)
    )
    prompt_acc = block_acc.reshape(requests, NEW, local_heads, HD)[inverse].reshape(
        row_count, local_heads, HD
    )
    own_prompt = rs_halving(
        (prompt_top, prompt_sum, prompt_acc), "seq", n_seq, halve_order, seq_index, combine_parts
    )
    home_query = lax.dynamic_slice_in_dim(query_req, seq_index * home_requests, home_requests, 0)
    home_pos = lax.dynamic_slice_in_dim(query_pos, seq_index * home_requests, home_requests, 0)
    home_prompt = lax.dynamic_slice_in_dim(req_prompt, seq_index * home_requests, home_requests, 0)
    home_filled = lax.dynamic_slice_in_dim(cont_len, seq_index * home_requests, home_requests, 0)
    cache_keys = cont_key.reshape(home_requests, slots, local_heads, HD)
    cache_vals = cont_val.reshape(home_requests, slots, local_heads, HD)
    slot_index = jnp.arange(slots, dtype=jnp.int32)
    cache_pos = home_prompt[:, None] + slot_index[None, :]
    cache_scores = (
        jnp.einsum("rjhd,rkhd->rhjk", home_query, cache_keys, preferred_element_type=jnp.float32)
        * score_scale
    )
    cache_scores = cache_scores + slopes[None, :, None, None] * (
        cache_pos[:, None, None, :] - home_pos[:, None, :, None]
    ).astype(jnp.float32)
    cache_live = (slot_index[None, :] < home_filled[:, None])[:, None, None, :]
    fresh_keys = key_new.reshape(home_requests, NEW, local_heads, HD)
    fresh_vals = val_new.reshape(home_requests, NEW, local_heads, HD)
    steps_new = jnp.arange(NEW, dtype=jnp.int32)
    fresh_dist = (steps_new[None, :] - steps_new[:, None]).astype(jnp.float32)
    fresh_scores = (
        jnp.einsum("rjhd,rkhd->rhjk", home_query, fresh_keys, preferred_element_type=jnp.float32)
        * score_scale
    )
    fresh_scores = fresh_scores + slopes[None, :, None, None] * fresh_dist[None, None, :, :]
    fresh_live = (steps_new[None, :] <= steps_new[:, None])[None, None, :, :]
    home_top = jnp.maximum(
        jnp.max(jnp.where(cache_live, cache_scores, NEG_FILL), -1),
        jnp.max(jnp.where(fresh_live, fresh_scores, NEG_FILL), -1),
    )
    cache_weights = jnp.where(cache_live, jnp.exp(cache_scores - home_top[..., None]), 0.0)
    fresh_weights = jnp.where(fresh_live, jnp.exp(fresh_scores - home_top[..., None]), 0.0)
    home_sum = jnp.sum(cache_weights, -1) + jnp.sum(fresh_weights, -1)
    home_acc = jnp.einsum(
        "rhjk,rkhd->rjhd",
        cache_weights.astype(jnp.bfloat16),
        cache_vals,
        preferred_element_type=jnp.float32,
    )
    home_acc = home_acc + jnp.einsum(
        "rhjk,rkhd->rjhd",
        fresh_weights.astype(jnp.bfloat16),
        fresh_vals,
        preferred_element_type=jnp.float32,
    )
    home_top = jnp.transpose(home_top, (0, 2, 1)).reshape(home_rows, local_heads)
    home_sum = jnp.transpose(home_sum, (0, 2, 1)).reshape(home_rows, local_heads)
    home_acc = home_acc.reshape(home_rows, local_heads, HD)
    merged = combine_parts(own_prompt, (home_top, home_sum, home_acc))
    own_attended = (
        (merged[2] / merged[1][..., None]).reshape(home_rows, feat_width).astype(jnp.bfloat16)
    )
    attended = ag_doubling(own_attended, "seq", n_seq, double_order, seq_index)
    attn_sum = ar_doubling(
        jnp.dot(attended, w_out, preferred_element_type=jnp.float32), "tp", n_tp, tp_bits
    )
    hidden_state = token_float + attn_sum
    second_stats = ar_doubling(
        jnp.stack([jnp.sum(hidden_state, 1), jnp.sum(hidden_state * hidden_state, 1)]),
        "seq", n_seq, halve_order,
    )
    second_normed = finish_norm(hidden_state, second_stats[0], second_stats[1], ln_second_gain)
    up_part = jnp.dot(second_normed, w_up, preferred_element_type=jnp.float32)
    (own_up,) = rs_halving((up_part,), "seq", n_seq, halve_order, seq_index, add_parts)
    own_activated = jax.nn.gelu(own_up, approximate=False).astype(jnp.bfloat16)
    activated = ag_doubling(own_activated, "seq", n_seq, double_order, seq_index)
    down_part = jnp.dot(activated, w_down, preferred_element_type=jnp.float32)
    down_sum = ar_doubling(down_part, "tp", n_tp, tp_bits)
    return (hidden_state + down_sum).astype(jnp.bfloat16)


def solution(mesh):
    in_specs = (
        P(None, "seq"),
        P("seq"),
        P("seq", None, "tp"),
        P("tp", "seq"),
        P("seq"),
        P("seq", "tp"),
        P("tp", "seq"),
        P(None, "seq", "tp"),
        P(None, "seq", "tp"),
        P("seq", None, "tp"),
        P("seq", None, "tp"),
        P(),
        P(),
        P(),
    )
    out_specs = P(None, "seq")
    return jax.shard_map(body, mesh=mesh, in_specs=in_specs, out_specs=out_specs, check_vma=False)
```

```python
import math

import jax
import jax.numpy as jnp
from jax import lax
from jax.sharding import PartitionSpec as P

D = 4096
HEADS = 32
HD = 128
NEW = 4


NEG_FILL = -1e30
NORM_EPS = 1e-05


def finish_norm(values, row_sum, row_square, gain):
    mean_row = row_sum / D
    variance = row_square / D - mean_row * mean_row
    scaled = (values - mean_row[:, None]) * lax.rsqrt(variance + NORM_EPS)[:, None]
    return (scaled * gain.astype(jnp.float32)[None, :]).astype(jnp.bfloat16)


def combine_parts(earlier, later):
    merged_top = jnp.maximum(earlier[0], later[0])
    left_factor = jnp.exp(earlier[0] - merged_top)
    right_factor = jnp.exp(later[0] - merged_top)
    merged_sum = earlier[1] * left_factor + later[1] * right_factor
    merged_acc = earlier[2] * left_factor[..., None] + later[2] * right_factor[..., None]
    return (merged_top, merged_sum, merged_acc)


def _levels(n):
    return n.bit_length() - 1


def _pairs(n, bit):
    return [(i, i ^ (1 << bit)) for i in range(n)]


def ar_doubling(x, axis, n, order):
    for bit in order:
        x = x + lax.ppermute(x, axis, _pairs(n, bit))
    return x


def add_parts(keep, got):
    return tuple(a + b for a, b in zip(keep, got))


def to_blocks(p, n):
    return p.reshape((2,) * _levels(n) + (p.shape[0] // n,) + p.shape[1:])


def rs_steps(parts, remaining, bits, axis, n, index, merge):
    remaining = list(remaining)
    for bit in bits:
        ax = remaining.index(bit)
        mine = (index >> bit) & 1
        keep = tuple(lax.dynamic_index_in_dim(p, mine, ax, keepdims=False) for p in parts)
        send = tuple(lax.dynamic_index_in_dim(p, 1 - mine, ax, keepdims=False) for p in parts)
        got = lax.ppermute(send, axis, _pairs(n, bit))
        parts = merge(keep, got)
        remaining.remove(bit)
    return parts, remaining


def rs_sum(x, axis, n, order, index, split):
    remaining = list(range(_levels(n) - 1, -1, -1))
    blocks = to_blocks(x, n)
    if split:
        half = x.shape[-1] // 2
        (low,), after = rs_steps((blocks[..., :half],), remaining, order[:2], axis, n, index, add_parts)
        (high,), _ = rs_steps((blocks[..., half:],), remaining, order[1::-1], axis, n, index, add_parts)
        blocks = jnp.concatenate([low, high], -1)
        remaining, order = after, order[2:]
    (out,), _ = rs_steps((blocks,), remaining, order, axis, n, index, add_parts)
    return out


def ag_steps(x, have, bits, axis, n, index):
    have = list(have)
    for bit in bits:
        got = lax.ppermute(x, axis, _pairs(n, bit))
        first = ((index >> bit) & 1) == 0
        low = jnp.where(first, x, got)
        high = jnp.where(first, got, x)
        pos = sum(1 for b in have if b > bit)
        x = jnp.stack([low, high], axis=pos)
        have.insert(pos, bit)
    return x, have


def ag_doubling(x, axis, n, order, index, split=False):
    levels = _levels(n)
    if split:
        x, have = ag_steps(x, [], order[:-2], axis, n, index)
        half = x.shape[-1] // 2
        low, _ = ag_steps(x[..., :half], have, order[-2:], axis, n, index)
        high, _ = ag_steps(x[..., half:], have, order[-2:][::-1], axis, n, index)
        x = jnp.concatenate([low, high], -1)
    else:
        x, _ = ag_steps(x, [], order, axis, n, index)
    return x.reshape((-1,) + x.shape[levels + 1 :])


def packed_merge(width, heads):
    def merge(keep, got):
        (mine,), (other,) = keep, got
        top = jnp.maximum(mine[..., width : width + heads], other[..., width : width + heads])
        mine_f = jnp.exp(mine[..., width : width + heads] - top)
        other_f = jnp.exp(other[..., width : width + heads] - top)
        total = mine[..., width + heads :] * mine_f + other[..., width + heads :] * other_f
        shape = mine.shape[:-1] + (heads, width // heads)
        acc = (
            mine[..., :width].reshape(shape) * mine_f[..., None]
            + other[..., :width].reshape(shape) * other_f[..., None]
        ).reshape(mine.shape[:-1] + (width,))
        return (jnp.concatenate([acc, top, total], -1),)

    return merge


def seq_orders(n):
    levels = _levels(n)
    near = [b for b in (0, 2, 1, 3, 4) if b < levels] + list(range(5, levels))
    return near, near[::-1]


def tp_order(n):
    return list(range(_levels(n)))


def body(
    tokens,
    ln_first_gain,
    w_qkv,
    w_out,
    ln_second_gain,
    w_up,
    w_down,
    prompt_key,
    prompt_val,
    cont_key,
    cont_val,
    group_ids,
    prompt_len,
    cont_len,
):
    row_count = tokens.shape[0]
    seq_index = lax.axis_index("seq")
    tp_index = lax.axis_index("tp")
    n_seq = lax.axis_size("seq")
    n_tp = lax.axis_size("tp")
    halve_order, double_order = seq_orders(n_seq)
    tp_bits = tp_order(n_tp)
    feat_width = w_qkv.shape[2]
    local_heads = feat_width // HD
    home_requests = cont_key.shape[0]
    home_rows = home_requests * NEW
    requests = row_count // NEW
    groups = prompt_key.shape[0]
    block_len = prompt_key.shape[1]
    slots = cont_key.shape[1]
    score_scale = 1.0 / math.sqrt(HD)
    token_float = tokens.astype(jnp.float32)
    first_stats = ar_doubling(
        jnp.stack([jnp.sum(token_float, 1), jnp.sum(token_float * token_float, 1)]),
        "seq", n_seq, halve_order,
    )
    normed = finish_norm(token_float, first_stats[0], first_stats[1], ln_first_gain)
    w_flat = w_qkv.reshape(w_qkv.shape[0], 3 * feat_width)
    partial_qkv = jnp.dot(normed, w_flat, preferred_element_type=jnp.float32)
    own_qkv = rs_sum(partial_qkv, "seq", n_seq, halve_order, seq_index, True)
    own_qkv = own_qkv.astype(jnp.bfloat16)
    query = ag_doubling(own_qkv[:, :feat_width], "seq", n_seq, double_order, seq_index)
    key_new = own_qkv[:, feat_width : 2 * feat_width]
    val_new = own_qkv[:, 2 * feat_width :]
    head_first = (tp_index * local_heads).astype(jnp.float32)
    slopes = jnp.exp2(
        -8.0 * (head_first + jnp.arange(local_heads, dtype=jnp.float32) + 1.0) / HEADS
    )
    members = jnp.argsort(group_ids, stable=True).reshape(groups, requests // groups)
    inverse = jnp.argsort(members.reshape(-1))
    group_match = group_ids[:, None] == jnp.arange(groups, dtype=jnp.int32)[None, :]
    req_prompt = jnp.sum(jnp.where(group_match, prompt_len[None, :], 0), 1)
    query_pos = (req_prompt + cont_len)[:, None] + jnp.arange(NEW, dtype=jnp.int32)[None, :]
    query_req = query.reshape(requests, NEW, local_heads, HD)
    group_query = query_req[members].reshape(groups, -1, local_heads, HD)
    group_pos = query_pos[members].reshape(groups, -1)
    key_slab = prompt_key.reshape(groups, block_len, local_heads, HD)
    val_slab = prompt_val.reshape(groups, block_len, local_heads, HD)
    key_pos = seq_index * block_len + jnp.arange(block_len, dtype=jnp.int32)
    scores = jnp.einsum(
        "gqhd,gphd->ghqp", group_query, key_slab, preferred_element_type=jnp.float32
    )
    distance = (key_pos[None, None, :] - group_pos[:, :, None]).astype(jnp.float32)
    scores = scores * score_scale + slopes[None, :, None, None] * distance[:, None, :, :]
    is_live = (key_pos[None, :] < prompt_len[:, None])[:, None, None, :]
    block_top = jnp.max(jnp.where(is_live, scores, NEG_FILL), -1)
    weights = jnp.where(is_live, jnp.exp(scores - block_top[..., None]), 0.0)
    block_sum = jnp.sum(weights, -1)
    block_acc = jnp.einsum(
        "ghqp,gphd->gqhd",
        weights.astype(jnp.bfloat16),
        val_slab,
        preferred_element_type=jnp.float32,
    )
    prompt_top = (
        jnp.transpose(block_top, (0, 2, 1))
        .reshape(requests, NEW, local_heads)[inverse]
        .reshape(row_count, local_heads)
    )
    prompt_sum = (
        jnp.transpose(block_sum, (0, 2, 1))
        .reshape(requests, NEW, local_heads)[inverse]
        .reshape(row_count, local_heads)
    )
    prompt_acc = block_acc.reshape(requests, NEW, local_heads, HD)[inverse].reshape(
        row_count, local_heads, HD
    )
    packed = jnp.concatenate(
        [prompt_acc.reshape(row_count, feat_width), prompt_top, prompt_sum], -1
    )
    remaining = list(range(_levels(n_seq) - 1, -1, -1))
    (packed,), _ = rs_steps(
        (to_blocks(packed, n_seq),), remaining, halve_order, "seq", n_seq, seq_index,
        packed_merge(feat_width, local_heads),
    )
    own_prompt = (
        packed[:, feat_width : feat_width + local_heads],
        packed[:, feat_width + local_heads :],
        packed[:, :feat_width].reshape(home_rows, local_heads, HD),
    )
    home_query = lax.dynamic_slice_in_dim(query_req, seq_index * home_requests, home_requests, 0)
    home_pos = lax.dynamic_slice_in_dim(query_pos, seq_index * home_requests, home_requests, 0)
    home_prompt = lax.dynamic_slice_in_dim(req_prompt, seq_index * home_requests, home_requests, 0)
    home_filled = lax.dynamic_slice_in_dim(cont_len, seq_index * home_requests, home_requests, 0)
    cache_keys = cont_key.reshape(home_requests, slots, local_heads, HD)
    cache_vals = cont_val.reshape(home_requests, slots, local_heads, HD)
    slot_index = jnp.arange(slots, dtype=jnp.int32)
    cache_pos = home_prompt[:, None] + slot_index[None, :]
    cache_scores = (
        jnp.einsum("rjhd,rkhd->rhjk", home_query, cache_keys, preferred_element_type=jnp.float32)
        * score_scale
    )
    cache_scores = cache_scores + slopes[None, :, None, None] * (
        cache_pos[:, None, None, :] - home_pos[:, None, :, None]
    ).astype(jnp.float32)
    cache_live = (slot_index[None, :] < home_filled[:, None])[:, None, None, :]
    fresh_keys = key_new.reshape(home_requests, NEW, local_heads, HD)
    fresh_vals = val_new.reshape(home_requests, NEW, local_heads, HD)
    steps_new = jnp.arange(NEW, dtype=jnp.int32)
    fresh_dist = (steps_new[None, :] - steps_new[:, None]).astype(jnp.float32)
    fresh_scores = (
        jnp.einsum("rjhd,rkhd->rhjk", home_query, fresh_keys, preferred_element_type=jnp.float32)
        * score_scale
    )
    fresh_scores = fresh_scores + slopes[None, :, None, None] * fresh_dist[None, None, :, :]
    fresh_live = (steps_new[None, :] <= steps_new[:, None])[None, None, :, :]
    home_top = jnp.maximum(
        jnp.max(jnp.where(cache_live, cache_scores, NEG_FILL), -1),
        jnp.max(jnp.where(fresh_live, fresh_scores, NEG_FILL), -1),
    )
    cache_weights = jnp.where(cache_live, jnp.exp(cache_scores - home_top[..., None]), 0.0)
    fresh_weights = jnp.where(fresh_live, jnp.exp(fresh_scores - home_top[..., None]), 0.0)
    home_sum = jnp.sum(cache_weights, -1) + jnp.sum(fresh_weights, -1)
    home_acc = jnp.einsum(
        "rhjk,rkhd->rjhd",
        cache_weights.astype(jnp.bfloat16),
        cache_vals,
        preferred_element_type=jnp.float32,
    )
    home_acc = home_acc + jnp.einsum(
        "rhjk,rkhd->rjhd",
        fresh_weights.astype(jnp.bfloat16),
        fresh_vals,
        preferred_element_type=jnp.float32,
    )
    home_top = jnp.transpose(home_top, (0, 2, 1)).reshape(home_rows, local_heads)
    home_sum = jnp.transpose(home_sum, (0, 2, 1)).reshape(home_rows, local_heads)
    home_acc = home_acc.reshape(home_rows, local_heads, HD)
    merged = combine_parts(own_prompt, (home_top, home_sum, home_acc))
    own_attended = (
        (merged[2] / merged[1][..., None]).reshape(home_rows, feat_width).astype(jnp.bfloat16)
    )
    attended = ag_doubling(own_attended, "seq", n_seq, double_order, seq_index)
    attn_sum = ar_doubling(
        jnp.dot(attended, w_out, preferred_element_type=jnp.float32), "tp", n_tp, tp_bits
    )
    hidden_state = token_float + attn_sum
    second_stats = ar_doubling(
        jnp.stack([jnp.sum(hidden_state, 1), jnp.sum(hidden_state * hidden_state, 1)]),
        "seq", n_seq, halve_order,
    )
    second_normed = finish_norm(hidden_state, second_stats[0], second_stats[1], ln_second_gain)
    up_part = jnp.dot(second_normed, w_up, preferred_element_type=jnp.float32)
    own_up = rs_sum(up_part, "seq", n_seq, halve_order, seq_index, True)
    own_activated = jax.nn.gelu(own_up, approximate=False).astype(jnp.bfloat16)
    activated = ag_doubling(own_activated, "seq", n_seq, double_order, seq_index, True)
    down_part = jnp.dot(activated, w_down, preferred_element_type=jnp.float32)
    down_sum = ar_doubling(down_part, "tp", n_tp, tp_bits)
    return (hidden_state + down_sum).astype(jnp.bfloat16)


def solution(mesh):
    in_specs = (
        P(None, "seq"),
        P("seq"),
        P("seq", None, "tp"),
        P("tp", "seq"),
        P("seq"),
        P("seq", "tp"),
        P("tp", "seq"),
        P(None, "seq", "tp"),
        P(None, "seq", "tp"),
        P("seq", None, "tp"),
        P("seq", None, "tp"),
        P(),
        P(),
        P(),
    )
    out_specs = P(None, "seq")
    return jax.shard_map(body, mesh=mesh, in_specs=in_specs, out_specs=out_specs, check_vma=False)
```

```python
import math

import jax
import jax.numpy as jnp
from jax import lax
from jax.sharding import PartitionSpec as P

D = 4096
HEADS = 32
HD = 128
NEW = 4


NEG_FILL = -1e30
NORM_EPS = 1e-05


def finish_norm(values, row_sum, row_square, gain):
    mean_row = row_sum / D
    variance = row_square / D - mean_row * mean_row
    scaled = (values - mean_row[:, None]) * lax.rsqrt(variance + NORM_EPS)[:, None]
    return (scaled * gain.astype(jnp.float32)[None, :]).astype(jnp.bfloat16)


def combine_parts(earlier, later):
    merged_top = jnp.maximum(earlier[0], later[0])
    left_factor = jnp.exp(earlier[0] - merged_top)
    right_factor = jnp.exp(later[0] - merged_top)
    merged_sum = earlier[1] * left_factor + later[1] * right_factor
    merged_acc = earlier[2] * left_factor[..., None] + later[2] * right_factor[..., None]
    return (merged_top, merged_sum, merged_acc)


def _levels(n):
    return n.bit_length() - 1


def _pairs(n, bit):
    return [(i, i ^ (1 << bit)) for i in range(n)]


def ar_doubling(x, axis, n, order):
    for bit in order:
        x = x + lax.ppermute(x, axis, _pairs(n, bit))
    return x


def add_parts(keep, got):
    return tuple(a + b for a, b in zip(keep, got))


def to_blocks(p, n):
    return p.reshape((2,) * _levels(n) + (p.shape[0] // n,) + p.shape[1:])


def rs_steps(parts, remaining, bits, axis, n, index, merge):
    remaining = list(remaining)
    for bit in bits:
        ax = remaining.index(bit)
        mine = (index >> bit) & 1
        keep = tuple(lax.dynamic_index_in_dim(p, mine, ax, keepdims=False) for p in parts)
        send = tuple(lax.dynamic_index_in_dim(p, 1 - mine, ax, keepdims=False) for p in parts)
        got = lax.ppermute(send, axis, _pairs(n, bit))
        parts = merge(keep, got)
        remaining.remove(bit)
    return parts, remaining


def rs_sum(x, axis, n, order, index, split):
    remaining = list(range(_levels(n) - 1, -1, -1))
    blocks = to_blocks(x, n)
    if split:
        half = x.shape[-1] // 2
        (low,), after = rs_steps((blocks[..., :half],), remaining, order[:2], axis, n, index, add_parts)
        (high,), _ = rs_steps((blocks[..., half:],), remaining, order[1::-1], axis, n, index, add_parts)
        blocks = jnp.concatenate([low, high], -1)
        remaining, order = after, order[2:]
    (out,), _ = rs_steps((blocks,), remaining, order, axis, n, index, add_parts)
    return out


def ag_steps(x, have, bits, axis, n, index):
    have = list(have)
    for bit in bits:
        got = lax.ppermute(x, axis, _pairs(n, bit))
        first = ((index >> bit) & 1) == 0
        low = jnp.where(first, x, got)
        high = jnp.where(first, got, x)
        pos = sum(1 for b in have if b > bit)
        x = jnp.stack([low, high], axis=pos)
        have.insert(pos, bit)
    return x, have


def ag_doubling(x, axis, n, order, index, split=False):
    levels = _levels(n)
    if split:
        x, have = ag_steps(x, [], order[:-2], axis, n, index)
        half = x.shape[-1] // 2
        low, _ = ag_steps(x[..., :half], have, order[-2:], axis, n, index)
        high, _ = ag_steps(x[..., half:], have, order[-2:][::-1], axis, n, index)
        x = jnp.concatenate([low, high], -1)
    else:
        x, _ = ag_steps(x, [], order, axis, n, index)
    return x.reshape((-1,) + x.shape[levels + 1 :])


def tiled_layout(n, rows, cols):
    levels = _levels(n)
    row_bits = levels - 1
    block_rows = rows >> row_bits
    shape = (2,) * row_bits + (block_rows, 2, cols // 2)
    layout = list(range(levels - 1, 0, -1)) + ["r", 0, "c"]
    return shape, layout


def rs_tiled(x, axis, n, order, index):
    shape, layout = tiled_layout(n, x.shape[0], x.shape[1])
    blocks = x.reshape(shape)
    quarter = shape[-1] // 2
    (low,), after = rs_steps((blocks[..., :quarter],), layout, order[:2], axis, n, index, add_parts)
    (high,), _ = rs_steps((blocks[..., quarter:],), layout, order[1::-1], axis, n, index, add_parts)
    (out,), _ = rs_steps((jnp.concatenate([low, high], -1),), after, order[2:], axis, n, index, add_parts)
    return out


def ag_place(x, have, bits, layout, axis, n, index):
    have = list(have)
    for bit in bits:
        got = lax.ppermute(x, axis, _pairs(n, bit))
        first = ((index >> bit) & 1) == 0
        low = jnp.where(first, x, got)
        high = jnp.where(first, got, x)
        rank = layout.index(bit)
        pos = sum(1 for b in have if layout.index(b) < rank)
        x = jnp.stack([low, high], axis=pos)
        have.insert(pos, bit)
    return x, have


def ag_tiled(x, axis, n, order, index, rows, cols):
    shape, layout = tiled_layout(n, rows, cols)
    x, have = ag_place(x, ["r", "c"], order[:-2], layout, axis, n, index)
    quarter = x.shape[-1] // 2
    low, _ = ag_place(x[..., :quarter], have, order[-2:], layout, axis, n, index)
    high, _ = ag_place(x[..., quarter:], have, order[-2:][::-1], layout, axis, n, index)
    return jnp.concatenate([low, high], -1).reshape(rows, cols)


def packed_merge(width, heads):
    def merge(keep, got):
        (mine,), (other,) = keep, got
        top = jnp.maximum(mine[..., width : width + heads], other[..., width : width + heads])
        mine_f = jnp.exp(mine[..., width : width + heads] - top)
        other_f = jnp.exp(other[..., width : width + heads] - top)
        total = mine[..., width + heads :] * mine_f + other[..., width + heads :] * other_f
        shape = mine.shape[:-1] + (heads, width // heads)
        acc = (
            mine[..., :width].reshape(shape) * mine_f[..., None]
            + other[..., :width].reshape(shape) * other_f[..., None]
        ).reshape(mine.shape[:-1] + (width,))
        return (jnp.concatenate([acc, top, total], -1),)

    return merge


def seq_orders(n):
    levels = _levels(n)
    near = [b for b in (0, 2, 1, 3, 4) if b < levels] + list(range(5, levels))
    return near, near[::-1]


def tp_order(n):
    return list(range(_levels(n)))


def body(
    tokens,
    ln_first_gain,
    w_qkv,
    w_out,
    ln_second_gain,
    w_up,
    w_down,
    prompt_key,
    prompt_val,
    cont_key,
    cont_val,
    group_ids,
    prompt_len,
    cont_len,
):
    row_count = tokens.shape[0]
    seq_index = lax.axis_index("seq")
    tp_index = lax.axis_index("tp")
    n_seq = lax.axis_size("seq")
    n_tp = lax.axis_size("tp")
    halve_order, double_order = seq_orders(n_seq)
    tp_bits = tp_order(n_tp)
    feat_width = w_qkv.shape[2]
    local_heads = feat_width // HD
    home_requests = cont_key.shape[0]
    home_rows = home_requests * NEW
    requests = row_count // NEW
    groups = prompt_key.shape[0]
    block_len = prompt_key.shape[1]
    slots = cont_key.shape[1]
    score_scale = 1.0 / math.sqrt(HD)
    token_float = tokens.astype(jnp.float32)
    first_stats = ar_doubling(
        jnp.stack([jnp.sum(token_float, 1), jnp.sum(token_float * token_float, 1)]),
        "seq", n_seq, halve_order,
    )
    normed = finish_norm(token_float, first_stats[0], first_stats[1], ln_first_gain)
    w_flat = w_qkv.reshape(w_qkv.shape[0], 3 * feat_width)
    partial_qkv = jnp.dot(normed, w_flat, preferred_element_type=jnp.float32)
    own_qkv = rs_sum(partial_qkv, "seq", n_seq, halve_order, seq_index, True)
    own_qkv = own_qkv.astype(jnp.bfloat16)
    query = ag_doubling(own_qkv[:, :feat_width], "seq", n_seq, double_order, seq_index)
    key_new = own_qkv[:, feat_width : 2 * feat_width]
    val_new = own_qkv[:, 2 * feat_width :]
    head_first = (tp_index * local_heads).astype(jnp.float32)
    slopes = jnp.exp2(
        -8.0 * (head_first + jnp.arange(local_heads, dtype=jnp.float32) + 1.0) / HEADS
    )
    members = jnp.argsort(group_ids, stable=True).reshape(groups, requests // groups)
    inverse = jnp.argsort(members.reshape(-1))
    group_match = group_ids[:, None] == jnp.arange(groups, dtype=jnp.int32)[None, :]
    req_prompt = jnp.sum(jnp.where(group_match, prompt_len[None, :], 0), 1)
    query_pos = (req_prompt + cont_len)[:, None] + jnp.arange(NEW, dtype=jnp.int32)[None, :]
    query_req = query.reshape(requests, NEW, local_heads, HD)
    group_query = query_req[members].reshape(groups, -1, local_heads, HD)
    group_pos = query_pos[members].reshape(groups, -1)
    key_slab = prompt_key.reshape(groups, block_len, local_heads, HD)
    val_slab = prompt_val.reshape(groups, block_len, local_heads, HD)
    key_pos = seq_index * block_len + jnp.arange(block_len, dtype=jnp.int32)
    scores = jnp.einsum(
        "gqhd,gphd->ghqp", group_query, key_slab, preferred_element_type=jnp.float32
    )
    distance = (key_pos[None, None, :] - group_pos[:, :, None]).astype(jnp.float32)
    scores = scores * score_scale + slopes[None, :, None, None] * distance[:, None, :, :]
    is_live = (key_pos[None, :] < prompt_len[:, None])[:, None, None, :]
    block_top = jnp.max(jnp.where(is_live, scores, NEG_FILL), -1)
    weights = jnp.where(is_live, jnp.exp(scores - block_top[..., None]), 0.0)
    block_sum = jnp.sum(weights, -1)
    block_acc = jnp.einsum(
        "ghqp,gphd->gqhd",
        weights.astype(jnp.bfloat16),
        val_slab,
        preferred_element_type=jnp.float32,
    )
    prompt_top = (
        jnp.transpose(block_top, (0, 2, 1))
        .reshape(requests, NEW, local_heads)[inverse]
        .reshape(row_count, local_heads)
    )
    prompt_sum = (
        jnp.transpose(block_sum, (0, 2, 1))
        .reshape(requests, NEW, local_heads)[inverse]
        .reshape(row_count, local_heads)
    )
    prompt_acc = block_acc.reshape(requests, NEW, local_heads, HD)[inverse].reshape(
        row_count, local_heads, HD
    )
    packed = jnp.concatenate(
        [prompt_acc.reshape(row_count, feat_width), prompt_top, prompt_sum], -1
    )
    remaining = list(range(_levels(n_seq) - 1, -1, -1))
    (packed,), _ = rs_steps(
        (to_blocks(packed, n_seq),), remaining, halve_order, "seq", n_seq, seq_index,
        packed_merge(feat_width, local_heads),
    )
    own_prompt = (
        packed[:, feat_width : feat_width + local_heads],
        packed[:, feat_width + local_heads :],
        packed[:, :feat_width].reshape(home_rows, local_heads, HD),
    )
    home_query = own_qkv[:, :feat_width].reshape(home_requests, NEW, local_heads, HD)
    home_pos = lax.dynamic_slice_in_dim(query_pos, seq_index * home_requests, home_requests, 0)
    home_prompt = lax.dynamic_slice_in_dim(req_prompt, seq_index * home_requests, home_requests, 0)
    home_filled = lax.dynamic_slice_in_dim(cont_len, seq_index * home_requests, home_requests, 0)
    cache_keys = cont_key.reshape(home_requests, slots, local_heads, HD)
    cache_vals = cont_val.reshape(home_requests, slots, local_heads, HD)
    slot_index = jnp.arange(slots, dtype=jnp.int32)
    cache_pos = home_prompt[:, None] + slot_index[None, :]
    cache_scores = (
        jnp.einsum("rjhd,rkhd->rhjk", home_query, cache_keys, preferred_element_type=jnp.float32)
        * score_scale
    )
    cache_scores = cache_scores + slopes[None, :, None, None] * (
        cache_pos[:, None, None, :] - home_pos[:, None, :, None]
    ).astype(jnp.float32)
    cache_live = (slot_index[None, :] < home_filled[:, None])[:, None, None, :]
    fresh_keys = key_new.reshape(home_requests, NEW, local_heads, HD)
    fresh_vals = val_new.reshape(home_requests, NEW, local_heads, HD)
    steps_new = jnp.arange(NEW, dtype=jnp.int32)
    fresh_dist = (steps_new[None, :] - steps_new[:, None]).astype(jnp.float32)
    fresh_scores = (
        jnp.einsum("rjhd,rkhd->rhjk", home_query, fresh_keys, preferred_element_type=jnp.float32)
        * score_scale
    )
    fresh_scores = fresh_scores + slopes[None, :, None, None] * fresh_dist[None, None, :, :]
    fresh_live = (steps_new[None, :] <= steps_new[:, None])[None, None, :, :]
    home_top = jnp.maximum(
        jnp.max(jnp.where(cache_live, cache_scores, NEG_FILL), -1),
        jnp.max(jnp.where(fresh_live, fresh_scores, NEG_FILL), -1),
    )
    cache_weights = jnp.where(cache_live, jnp.exp(cache_scores - home_top[..., None]), 0.0)
    fresh_weights = jnp.where(fresh_live, jnp.exp(fresh_scores - home_top[..., None]), 0.0)
    home_sum = jnp.sum(cache_weights, -1) + jnp.sum(fresh_weights, -1)
    home_acc = jnp.einsum(
        "rhjk,rkhd->rjhd",
        cache_weights.astype(jnp.bfloat16),
        cache_vals,
        preferred_element_type=jnp.float32,
    )
    home_acc = home_acc + jnp.einsum(
        "rhjk,rkhd->rjhd",
        fresh_weights.astype(jnp.bfloat16),
        fresh_vals,
        preferred_element_type=jnp.float32,
    )
    home_top = jnp.transpose(home_top, (0, 2, 1)).reshape(home_rows, local_heads)
    home_sum = jnp.transpose(home_sum, (0, 2, 1)).reshape(home_rows, local_heads)
    home_acc = home_acc.reshape(home_rows, local_heads, HD)
    merged = combine_parts(own_prompt, (home_top, home_sum, home_acc))
    own_attended = (
        (merged[2] / merged[1][..., None]).reshape(home_rows, feat_width).astype(jnp.bfloat16)
    )
    attended = ag_doubling(own_attended, "seq", n_seq, double_order, seq_index)
    attn_sum = ar_doubling(
        jnp.dot(attended, w_out, preferred_element_type=jnp.float32), "tp", n_tp, tp_bits
    )
    hidden_state = token_float + attn_sum
    second_stats = ar_doubling(
        jnp.stack([jnp.sum(hidden_state, 1), jnp.sum(hidden_state * hidden_state, 1)]),
        "seq", n_seq, halve_order,
    )
    second_normed = finish_norm(hidden_state, second_stats[0], second_stats[1], ln_second_gain)
    up_part = jnp.dot(second_normed, w_up, preferred_element_type=jnp.float32)
    own_up = rs_tiled(up_part, "seq", n_seq, halve_order, seq_index)
    own_activated = jax.nn.gelu(own_up, approximate=False).astype(jnp.bfloat16)
    activated = ag_tiled(
        own_activated, "seq", n_seq, double_order, seq_index, up_part.shape[0], up_part.shape[1]
    )
    down_part = jnp.dot(activated, w_down, preferred_element_type=jnp.float32)
    down_sum = ar_doubling(down_part, "tp", n_tp, tp_bits)
    return (hidden_state + down_sum).astype(jnp.bfloat16)


def solution(mesh):
    in_specs = (
        P(None, "seq"),
        P("seq"),
        P("seq", None, "tp"),
        P("tp", "seq"),
        P("seq"),
        P("seq", "tp"),
        P("tp", "seq"),
        P(None, "seq", "tp"),
        P(None, "seq", "tp"),
        P("seq", None, "tp"),
        P("seq", None, "tp"),
        P(),
        P(),
        P(),
    )
    out_specs = P(None, "seq")
    return jax.shard_map(body, mesh=mesh, in_specs=in_specs, out_specs=out_specs, check_vma=False)
```

```python
import math

import jax
import jax.numpy as jnp
from jax import lax
from jax.sharding import PartitionSpec as P

D = 4096
HEADS = 32
HD = 128
NEW = 4


NEG_FILL = -1e30
NORM_EPS = 1e-05


def finish_norm(values, row_sum, row_square, gain):
    mean_row = row_sum / D
    variance = row_square / D - mean_row * mean_row
    scaled = (values - mean_row[:, None]) * lax.rsqrt(variance + NORM_EPS)[:, None]
    return (scaled * gain.astype(jnp.float32)[None, :]).astype(jnp.bfloat16)


def combine_parts(earlier, later):
    merged_top = jnp.maximum(earlier[0], later[0])
    left_factor = jnp.exp(earlier[0] - merged_top)
    right_factor = jnp.exp(later[0] - merged_top)
    merged_sum = earlier[1] * left_factor + later[1] * right_factor
    merged_acc = earlier[2] * left_factor[..., None] + later[2] * right_factor[..., None]
    return (merged_top, merged_sum, merged_acc)


def _levels(n):
    return n.bit_length() - 1


def _pairs(n, bit):
    return [(i, i ^ (1 << bit)) for i in range(n)]


def ar_doubling(x, axis, n, order):
    for bit in order:
        x = x + lax.ppermute(x, axis, _pairs(n, bit))
    return x


def add_parts(keep, got):
    return tuple(a + b for a, b in zip(keep, got))


def to_blocks(p, n):
    return p.reshape((2,) * _levels(n) + (p.shape[0] // n,) + p.shape[1:])


def rs_steps(parts, remaining, bits, axis, n, index, merge):
    remaining = list(remaining)
    for bit in bits:
        ax = remaining.index(bit)
        mine = (index >> bit) & 1
        keep = tuple(lax.dynamic_index_in_dim(p, mine, ax, keepdims=False) for p in parts)
        send = tuple(lax.dynamic_index_in_dim(p, 1 - mine, ax, keepdims=False) for p in parts)
        got = lax.ppermute(send, axis, _pairs(n, bit))
        parts = merge(keep, got)
        remaining.remove(bit)
    return parts, remaining


def rs_sum(x, axis, n, order, index, split):
    remaining = list(range(_levels(n) - 1, -1, -1))
    blocks = to_blocks(x, n)
    if split:
        half = x.shape[-1] // 2
        (low,), after = rs_steps((blocks[..., :half],), remaining, order[:2], axis, n, index, add_parts)
        (high,), _ = rs_steps((blocks[..., half:],), remaining, order[1::-1], axis, n, index, add_parts)
        blocks = jnp.concatenate([low, high], -1)
        remaining, order = after, order[2:]
    (out,), _ = rs_steps((blocks,), remaining, order, axis, n, index, add_parts)
    return out


def ag_steps(x, have, bits, axis, n, index):
    have = list(have)
    for bit in bits:
        got = lax.ppermute(x, axis, _pairs(n, bit))
        first = ((index >> bit) & 1) == 0
        low = jnp.where(first, x, got)
        high = jnp.where(first, got, x)
        pos = sum(1 for b in have if b > bit)
        x = jnp.stack([low, high], axis=pos)
        have.insert(pos, bit)
    return x, have


def ag_doubling(x, axis, n, order, index, split=False):
    levels = _levels(n)
    if split:
        x, have = ag_steps(x, [], order[:-2], axis, n, index)
        half = x.shape[-1] // 2
        low, _ = ag_steps(x[..., :half], have, order[-2:], axis, n, index)
        high, _ = ag_steps(x[..., half:], have, order[-2:][::-1], axis, n, index)
        x = jnp.concatenate([low, high], -1)
    else:
        x, _ = ag_steps(x, [], order, axis, n, index)
    return x.reshape((-1,) + x.shape[levels + 1 :])


def tiled_layout(n, rows, cols):
    levels = _levels(n)
    row_bits = levels - 1
    shape = (2,) + (2,) * row_bits + (rows >> row_bits, cols)
    layout = [0] + list(range(levels - 1, 0, -1)) + ["r", "c"]
    return shape, layout


def rs_tiled(x, axis, n, order, index):
    shape, layout = tiled_layout(n, x.shape[1], x.shape[2])
    blocks = x.reshape(shape)
    top_bit = _levels(n) - 1
    cut = layout.index(top_bit)
    low = lax.slice_in_dim(blocks, 0, 1, axis=cut)
    high = lax.slice_in_dim(blocks, 1, 2, axis=cut)
    (low,), after = rs_steps((low,), layout, order[:2], axis, n, index, add_parts)
    (high,), _ = rs_steps((high,), layout, order[1::-1], axis, n, index, add_parts)
    joined = jnp.concatenate([low, high], after.index(top_bit))
    (out,), _ = rs_steps((joined,), after, order[2:], axis, n, index, add_parts)
    return out


def ag_place(x, have, bits, layout, axis, n, index):
    have = list(have)
    for bit in bits:
        got = lax.ppermute(x, axis, _pairs(n, bit))
        first = ((index >> bit) & 1) == 0
        low = jnp.where(first, x, got)
        high = jnp.where(first, got, x)
        rank = layout.index(bit)
        pos = sum(1 for b in have if layout.index(b) < rank)
        x = jnp.stack([low, high], axis=pos)
        have.insert(pos, bit)
    return x, have


def ag_tiled(x, axis, n, order, index, rows, cols):
    shape, layout = tiled_layout(n, rows, cols)
    top_bit = _levels(n) - 1
    x, have = ag_place(x, ["r", "c"], order[:-2], layout, axis, n, index)
    cut = have.index(top_bit)
    low, done = ag_place(
        lax.slice_in_dim(x, 0, 1, axis=cut), have, order[-2:], layout, axis, n, index
    )
    high, _ = ag_place(
        lax.slice_in_dim(x, 1, 2, axis=cut), have, order[-2:][::-1], layout, axis, n, index
    )
    joined = jnp.concatenate([low, high], done.index(top_bit))
    return joined.reshape(2, rows, cols)


def packed_merge(width, heads):
    def merge(keep, got):
        (mine,), (other,) = keep, got
        top = jnp.maximum(mine[..., width : width + heads], other[..., width : width + heads])
        mine_f = jnp.exp(mine[..., width : width + heads] - top)
        other_f = jnp.exp(other[..., width : width + heads] - top)
        total = mine[..., width + heads :] * mine_f + other[..., width + heads :] * other_f
        shape = mine.shape[:-1] + (heads, width // heads)
        acc = (
            mine[..., :width].reshape(shape) * mine_f[..., None]
            + other[..., :width].reshape(shape) * other_f[..., None]
        ).reshape(mine.shape[:-1] + (width,))
        return (jnp.concatenate([acc, top, total], -1),)

    return merge


def seq_orders(n):
    levels = _levels(n)
    near = [b for b in (0, 2, 1, 3, 4) if b < levels] + list(range(5, levels))
    return near, near[::-1]


def tp_order(n):
    return list(range(_levels(n)))


def body(
    tokens,
    ln_first_gain,
    w_qkv,
    w_out,
    ln_second_gain,
    w_up,
    w_down,
    prompt_key,
    prompt_val,
    cont_key,
    cont_val,
    group_ids,
    prompt_len,
    cont_len,
):
    row_count = tokens.shape[0]
    seq_index = lax.axis_index("seq")
    tp_index = lax.axis_index("tp")
    n_seq = lax.axis_size("seq")
    n_tp = lax.axis_size("tp")
    halve_order, double_order = seq_orders(n_seq)
    tp_bits = tp_order(n_tp)
    feat_width = w_qkv.shape[2]
    local_heads = feat_width // HD
    home_requests = cont_key.shape[0]
    home_rows = home_requests * NEW
    requests = row_count // NEW
    groups = prompt_key.shape[0]
    block_len = prompt_key.shape[1]
    slots = cont_key.shape[1]
    score_scale = 1.0 / math.sqrt(HD)
    token_float = tokens.astype(jnp.float32)
    first_stats = ar_doubling(
        jnp.stack([jnp.sum(token_float, 1), jnp.sum(token_float * token_float, 1)]),
        "seq", n_seq, halve_order,
    )
    normed = finish_norm(token_float, first_stats[0], first_stats[1], ln_first_gain)
    w_flat = w_qkv.reshape(w_qkv.shape[0], 3 * feat_width)
    partial_qkv = jnp.dot(normed, w_flat, preferred_element_type=jnp.float32)
    own_qkv = rs_sum(partial_qkv, "seq", n_seq, halve_order, seq_index, True)
    own_qkv = own_qkv.astype(jnp.bfloat16)
    query = ag_doubling(own_qkv[:, :feat_width], "seq", n_seq, double_order, seq_index)
    key_new = own_qkv[:, feat_width : 2 * feat_width]
    val_new = own_qkv[:, 2 * feat_width :]
    head_first = (tp_index * local_heads).astype(jnp.float32)
    slopes = jnp.exp2(
        -8.0 * (head_first + jnp.arange(local_heads, dtype=jnp.float32) + 1.0) / HEADS
    )
    members = jnp.argsort(group_ids, stable=True).reshape(groups, requests // groups)
    inverse = jnp.argsort(members.reshape(-1))
    group_match = group_ids[:, None] == jnp.arange(groups, dtype=jnp.int32)[None, :]
    req_prompt = jnp.sum(jnp.where(group_match, prompt_len[None, :], 0), 1)
    query_pos = (req_prompt + cont_len)[:, None] + jnp.arange(NEW, dtype=jnp.int32)[None, :]
    query_req = query.reshape(requests, NEW, local_heads, HD)
    group_query = query_req[members].reshape(groups, -1, local_heads, HD)
    group_pos = query_pos[members].reshape(groups, -1)
    key_slab = prompt_key.reshape(groups, block_len, local_heads, HD)
    val_slab = prompt_val.reshape(groups, block_len, local_heads, HD)
    key_pos = seq_index * block_len + jnp.arange(block_len, dtype=jnp.int32)
    scores = jnp.einsum(
        "gqhd,gphd->ghqp", group_query, key_slab, preferred_element_type=jnp.float32
    )
    distance = (key_pos[None, None, :] - group_pos[:, :, None]).astype(jnp.float32)
    scores = scores * score_scale + slopes[None, :, None, None] * distance[:, None, :, :]
    is_live = (key_pos[None, :] < prompt_len[:, None])[:, None, None, :]
    block_top = jnp.max(jnp.where(is_live, scores, NEG_FILL), -1)
    weights = jnp.where(is_live, jnp.exp(scores - block_top[..., None]), 0.0)
    block_sum = jnp.sum(weights, -1)
    block_acc = jnp.einsum(
        "ghqp,gphd->gqhd",
        weights.astype(jnp.bfloat16),
        val_slab,
        preferred_element_type=jnp.float32,
    )
    prompt_top = (
        jnp.transpose(block_top, (0, 2, 1))
        .reshape(requests, NEW, local_heads)[inverse]
        .reshape(row_count, local_heads)
    )
    prompt_sum = (
        jnp.transpose(block_sum, (0, 2, 1))
        .reshape(requests, NEW, local_heads)[inverse]
        .reshape(row_count, local_heads)
    )
    prompt_acc = block_acc.reshape(requests, NEW, local_heads, HD)[inverse].reshape(
        row_count, local_heads, HD
    )
    packed = jnp.concatenate(
        [prompt_acc.reshape(row_count, feat_width), prompt_top, prompt_sum], -1
    )
    remaining = list(range(_levels(n_seq) - 1, -1, -1))
    (packed,), _ = rs_steps(
        (to_blocks(packed, n_seq),), remaining, halve_order, "seq", n_seq, seq_index,
        packed_merge(feat_width, local_heads),
    )
    own_prompt = (
        packed[:, feat_width : feat_width + local_heads],
        packed[:, feat_width + local_heads :],
        packed[:, :feat_width].reshape(home_rows, local_heads, HD),
    )
    home_query = own_qkv[:, :feat_width].reshape(home_requests, NEW, local_heads, HD)
    home_pos = lax.dynamic_slice_in_dim(query_pos, seq_index * home_requests, home_requests, 0)
    home_prompt = lax.dynamic_slice_in_dim(req_prompt, seq_index * home_requests, home_requests, 0)
    home_filled = lax.dynamic_slice_in_dim(cont_len, seq_index * home_requests, home_requests, 0)
    cache_keys = cont_key.reshape(home_requests, slots, local_heads, HD)
    cache_vals = cont_val.reshape(home_requests, slots, local_heads, HD)
    slot_index = jnp.arange(slots, dtype=jnp.int32)
    cache_pos = home_prompt[:, None] + slot_index[None, :]
    cache_scores = (
        jnp.einsum("rjhd,rkhd->rhjk", home_query, cache_keys, preferred_element_type=jnp.float32)
        * score_scale
    )
    cache_scores = cache_scores + slopes[None, :, None, None] * (
        cache_pos[:, None, None, :] - home_pos[:, None, :, None]
    ).astype(jnp.float32)
    cache_live = (slot_index[None, :] < home_filled[:, None])[:, None, None, :]
    fresh_keys = key_new.reshape(home_requests, NEW, local_heads, HD)
    fresh_vals = val_new.reshape(home_requests, NEW, local_heads, HD)
    steps_new = jnp.arange(NEW, dtype=jnp.int32)
    fresh_dist = (steps_new[None, :] - steps_new[:, None]).astype(jnp.float32)
    fresh_scores = (
        jnp.einsum("rjhd,rkhd->rhjk", home_query, fresh_keys, preferred_element_type=jnp.float32)
        * score_scale
    )
    fresh_scores = fresh_scores + slopes[None, :, None, None] * fresh_dist[None, None, :, :]
    fresh_live = (steps_new[None, :] <= steps_new[:, None])[None, None, :, :]
    home_top = jnp.maximum(
        jnp.max(jnp.where(cache_live, cache_scores, NEG_FILL), -1),
        jnp.max(jnp.where(fresh_live, fresh_scores, NEG_FILL), -1),
    )
    cache_weights = jnp.where(cache_live, jnp.exp(cache_scores - home_top[..., None]), 0.0)
    fresh_weights = jnp.where(fresh_live, jnp.exp(fresh_scores - home_top[..., None]), 0.0)
    home_sum = jnp.sum(cache_weights, -1) + jnp.sum(fresh_weights, -1)
    home_acc = jnp.einsum(
        "rhjk,rkhd->rjhd",
        cache_weights.astype(jnp.bfloat16),
        cache_vals,
        preferred_element_type=jnp.float32,
    )
    home_acc = home_acc + jnp.einsum(
        "rhjk,rkhd->rjhd",
        fresh_weights.astype(jnp.bfloat16),
        fresh_vals,
        preferred_element_type=jnp.float32,
    )
    home_top = jnp.transpose(home_top, (0, 2, 1)).reshape(home_rows, local_heads)
    home_sum = jnp.transpose(home_sum, (0, 2, 1)).reshape(home_rows, local_heads)
    home_acc = home_acc.reshape(home_rows, local_heads, HD)
    merged = combine_parts(own_prompt, (home_top, home_sum, home_acc))
    own_attended = (
        (merged[2] / merged[1][..., None]).reshape(home_rows, feat_width).astype(jnp.bfloat16)
    )
    attended = ag_doubling(own_attended, "seq", n_seq, double_order, seq_index)
    attn_sum = ar_doubling(
        jnp.dot(attended, w_out, preferred_element_type=jnp.float32), "tp", n_tp, tp_bits
    )
    hidden_state = token_float + attn_sum
    second_stats = ar_doubling(
        jnp.stack([jnp.sum(hidden_state, 1), jnp.sum(hidden_state * hidden_state, 1)]),
        "seq", n_seq, halve_order,
    )
    second_normed = finish_norm(hidden_state, second_stats[0], second_stats[1], ln_second_gain)
    halves = w_up.shape[1] // 2
    up_part = jnp.einsum(
        "rk,kcn->crn",
        second_normed,
        w_up.reshape(w_up.shape[0], 2, halves),
        preferred_element_type=jnp.float32,
    )
    own_up = rs_tiled(up_part, "seq", n_seq, halve_order, seq_index)
    own_activated = jax.nn.gelu(own_up, approximate=False).astype(jnp.bfloat16)
    activated = ag_tiled(own_activated, "seq", n_seq, double_order, seq_index, row_count, halves)
    down_part = jnp.einsum(
        "crn,cnf->rf",
        activated,
        w_down.reshape(2, halves, w_down.shape[1]),
        preferred_element_type=jnp.float32,
    )
    down_sum = ar_doubling(down_part, "tp", n_tp, tp_bits)
    return (hidden_state + down_sum).astype(jnp.bfloat16)


def solution(mesh):
    in_specs = (
        P(None, "seq"),
        P("seq"),
        P("seq", None, "tp"),
        P("tp", "seq"),
        P("seq"),
        P("seq", "tp"),
        P("tp", "seq"),
        P(None, "seq", "tp"),
        P(None, "seq", "tp"),
        P("seq", None, "tp"),
        P("seq", None, "tp"),
        P(),
        P(),
        P(),
    )
    out_specs = P(None, "seq")
    return jax.shard_map(body, mesh=mesh, in_specs=in_specs, out_specs=out_specs, check_vma=False)
```

```python
import math

import jax
import jax.numpy as jnp
from jax import lax
from jax.sharding import PartitionSpec as P

D = 4096
HEADS = 32
HD = 128
NEW = 4


NEG_FILL = -1e30
NORM_EPS = 1e-05


def finish_norm(values, row_sum, row_square, gain):
    mean_row = row_sum / D
    variance = row_square / D - mean_row * mean_row
    scaled = (values - mean_row[:, None]) * lax.rsqrt(variance + NORM_EPS)[:, None]
    return (scaled * gain.astype(jnp.float32)[None, :]).astype(jnp.bfloat16)


def combine_parts(earlier, later):
    merged_top = jnp.maximum(earlier[0], later[0])
    left_factor = jnp.exp(earlier[0] - merged_top)
    right_factor = jnp.exp(later[0] - merged_top)
    merged_sum = earlier[1] * left_factor + later[1] * right_factor
    merged_acc = earlier[2] * left_factor[..., None] + later[2] * right_factor[..., None]
    return (merged_top, merged_sum, merged_acc)


def _levels(n):
    return n.bit_length() - 1


def _pairs(n, bit):
    return [(i, i ^ (1 << bit)) for i in range(n)]


def ar_doubling(x, axis, n, order):
    for bit in order:
        x = x + lax.ppermute(x, axis, _pairs(n, bit))
    return x


def add_parts(keep, got):
    return tuple(a + b for a, b in zip(keep, got))


def to_blocks(p, n):
    return p.reshape((2,) * _levels(n) + (p.shape[0] // n,) + p.shape[1:])


def rs_steps(parts, remaining, bits, axis, n, index, merge):
    remaining = list(remaining)
    for bit in bits:
        ax = remaining.index(bit)
        mine = (index >> bit) & 1
        keep = tuple(lax.dynamic_index_in_dim(p, mine, ax, keepdims=False) for p in parts)
        send = tuple(lax.dynamic_index_in_dim(p, 1 - mine, ax, keepdims=False) for p in parts)
        got = lax.ppermute(send, axis, _pairs(n, bit))
        parts = merge(keep, got)
        remaining.remove(bit)
    return parts, remaining


def rs_sum(x, axis, n, order, index, split):
    remaining = list(range(_levels(n) - 1, -1, -1))
    blocks = to_blocks(x, n)
    if split:
        half = x.shape[-1] // 2
        (low,), after = rs_steps((blocks[..., :half],), remaining, order[:2], axis, n, index, add_parts)
        (high,), _ = rs_steps((blocks[..., half:],), remaining, order[1::-1], axis, n, index, add_parts)
        blocks = jnp.concatenate([low, high], -1)
        remaining, order = after, order[2:]
    (out,), _ = rs_steps((blocks,), remaining, order, axis, n, index, add_parts)
    return out


def ag_steps(x, have, bits, axis, n, index):
    have = list(have)
    for bit in bits:
        got = lax.ppermute(x, axis, _pairs(n, bit))
        first = ((index >> bit) & 1) == 0
        low = jnp.where(first, x, got)
        high = jnp.where(first, got, x)
        pos = sum(1 for b in have if b > bit)
        x = jnp.stack([low, high], axis=pos)
        have.insert(pos, bit)
    return x, have


def ag_doubling(x, axis, n, order, index, split=False):
    levels = _levels(n)
    if split:
        x, have = ag_steps(x, [], order[:-2], axis, n, index)
        half = x.shape[-1] // 2
        low, _ = ag_steps(x[..., :half], have, order[-2:], axis, n, index)
        high, _ = ag_steps(x[..., half:], have, order[-2:][::-1], axis, n, index)
        x = jnp.concatenate([low, high], -1)
    else:
        x, _ = ag_steps(x, [], order, axis, n, index)
    return x.reshape((-1,) + x.shape[levels + 1 :])


def tiled_layout(n, rows, cols):
    levels = _levels(n)
    row_bits = levels - 1
    shape = (2,) + (2,) * row_bits + (rows >> row_bits, cols)
    layout = [0] + list(range(levels - 1, 0, -1)) + ["r", "c"]
    return shape, layout


def rs_tiled(x, axis, n, order, index):
    shape, layout = tiled_layout(n, x.shape[1], x.shape[2])
    blocks = x.reshape(shape)
    top_bit = _levels(n) - 1
    cut = layout.index(top_bit)
    low = lax.slice_in_dim(blocks, 0, 1, axis=cut)
    high = lax.slice_in_dim(blocks, 1, 2, axis=cut)
    (low,), after = rs_steps((low,), layout, order[:2], axis, n, index, add_parts)
    (high,), _ = rs_steps((high,), layout, order[1::-1], axis, n, index, add_parts)
    joined = jnp.concatenate([low, high], after.index(top_bit))
    (out,), _ = rs_steps((joined,), after, order[2:], axis, n, index, add_parts)
    return out


def ag_place(x, have, bits, layout, axis, n, index):
    have = list(have)
    for bit in bits:
        got = lax.ppermute(x, axis, _pairs(n, bit))
        first = ((index >> bit) & 1) == 0
        low = jnp.where(first, x, got)
        high = jnp.where(first, got, x)
        rank = layout.index(bit)
        pos = sum(1 for b in have if layout.index(b) < rank)
        x = jnp.stack([low, high], axis=pos)
        have.insert(pos, bit)
    return x, have


def ag_tiled(x, axis, n, order, index, rows, cols):
    shape, layout = tiled_layout(n, rows, cols)
    top_bit = _levels(n) - 1
    x, have = ag_place(x, ["r", "c"], order[:-2], layout, axis, n, index)
    cut = have.index(top_bit)
    low, done = ag_place(
        lax.slice_in_dim(x, 0, 1, axis=cut), have, order[-2:], layout, axis, n, index
    )
    high, _ = ag_place(
        lax.slice_in_dim(x, 1, 2, axis=cut), have, order[-2:][::-1], layout, axis, n, index
    )
    joined = jnp.concatenate([low, high], done.index(top_bit))
    return joined.reshape(2, rows, cols)


def rs_two_link(blocks, layout, order, axis, n, index, merge):
    top_bit = _levels(n) - 1
    cut = layout.index(top_bit)
    low = tuple(lax.slice_in_dim(p, 0, 1, axis=cut) for p in blocks)
    high = tuple(lax.slice_in_dim(p, 1, 2, axis=cut) for p in blocks)
    low, after = rs_steps(low, layout, order[:2], axis, n, index, merge)
    high, _ = rs_steps(high, layout, order[1::-1], axis, n, index, merge)
    at = after.index(top_bit)
    joined = tuple(jnp.concatenate([a, b], at) for a, b in zip(low, high))
    out, _ = rs_steps(joined, after, order[2:], axis, n, index, merge)
    return out


def stable_ranks(keys):
    count = keys.shape[0]
    order = jnp.arange(count, dtype=jnp.int32)
    before = (keys[None, :] < keys[:, None]) | (
        (keys[None, :] == keys[:, None]) & (order[None, :] < order[:, None])
    )
    rank = jnp.sum(before.astype(jnp.int32), 1)
    placed = jnp.sum(jnp.where(rank[None, :] == order[:, None], order[None, :], 0), 1)
    return placed, rank


def packed_merge(width, heads):
    def merge(keep, got):
        (mine,), (other,) = keep, got
        top = jnp.maximum(mine[..., width : width + heads], other[..., width : width + heads])
        mine_f = jnp.exp(mine[..., width : width + heads] - top)
        other_f = jnp.exp(other[..., width : width + heads] - top)
        total = mine[..., width + heads :] * mine_f + other[..., width + heads :] * other_f
        shape = mine.shape[:-1] + (heads, width // heads)
        acc = (
            mine[..., :width].reshape(shape) * mine_f[..., None]
            + other[..., :width].reshape(shape) * other_f[..., None]
        ).reshape(mine.shape[:-1] + (width,))
        return (jnp.concatenate([acc, top, total], -1),)

    return merge


def seq_orders(n):
    levels = _levels(n)
    near = [b for b in (0, 2, 1, 3, 4) if b < levels] + list(range(5, levels))
    return near, near[::-1]


def tp_order(n):
    return list(range(_levels(n)))


def body(
    tokens,
    ln_first_gain,
    w_qkv,
    w_out,
    ln_second_gain,
    w_up,
    w_down,
    prompt_key,
    prompt_val,
    cont_key,
    cont_val,
    group_ids,
    prompt_len,
    cont_len,
):
    row_count = tokens.shape[0]
    seq_index = lax.axis_index("seq")
    tp_index = lax.axis_index("tp")
    n_seq = lax.axis_size("seq")
    n_tp = lax.axis_size("tp")
    halve_order, double_order = seq_orders(n_seq)
    tp_bits = tp_order(n_tp)
    feat_width = w_qkv.shape[2]
    local_heads = feat_width // HD
    home_requests = cont_key.shape[0]
    home_rows = home_requests * NEW
    requests = row_count // NEW
    groups = prompt_key.shape[0]
    block_len = prompt_key.shape[1]
    slots = cont_key.shape[1]
    score_scale = 1.0 / math.sqrt(HD)
    token_float = tokens.astype(jnp.float32)
    first_stats = ar_doubling(
        jnp.stack([jnp.sum(token_float, 1), jnp.sum(token_float * token_float, 1)]),
        "seq", n_seq, halve_order,
    )
    normed = finish_norm(token_float, first_stats[0], first_stats[1], ln_first_gain)
    w_flat = w_qkv.reshape(w_qkv.shape[0], 3 * feat_width)
    partial_qkv = jnp.dot(normed, w_flat, preferred_element_type=jnp.float32)
    seq_layout = list(range(_levels(n_seq) - 1, -1, -1)) + ["r", "c"]
    (own_qkv,) = rs_two_link(
        (to_blocks(partial_qkv, n_seq),), seq_layout, halve_order, "seq", n_seq, seq_index, add_parts
    )
    own_qkv = own_qkv.astype(jnp.bfloat16)
    query = ag_doubling(own_qkv[:, :feat_width], "seq", n_seq, double_order, seq_index)
    key_new = own_qkv[:, feat_width : 2 * feat_width]
    val_new = own_qkv[:, 2 * feat_width :]
    head_first = (tp_index * local_heads).astype(jnp.float32)
    slopes = jnp.exp2(
        -8.0 * (head_first + jnp.arange(local_heads, dtype=jnp.float32) + 1.0) / HEADS
    )
    placed, inverse = stable_ranks(group_ids)
    members = placed.reshape(groups, requests // groups)
    group_match = group_ids[:, None] == jnp.arange(groups, dtype=jnp.int32)[None, :]
    req_prompt = jnp.sum(jnp.where(group_match, prompt_len[None, :], 0), 1)
    query_pos = (req_prompt + cont_len)[:, None] + jnp.arange(NEW, dtype=jnp.int32)[None, :]
    query_req = query.reshape(requests, NEW, local_heads, HD)
    group_query = query_req[members].reshape(groups, -1, local_heads, HD)
    group_pos = query_pos[members].reshape(groups, -1)
    key_slab = prompt_key.reshape(groups, block_len, local_heads, HD)
    val_slab = prompt_val.reshape(groups, block_len, local_heads, HD)
    key_pos = seq_index * block_len + jnp.arange(block_len, dtype=jnp.int32)
    scores = jnp.einsum(
        "gqhd,gphd->ghqp", group_query, key_slab, preferred_element_type=jnp.float32
    )
    distance = (key_pos[None, None, :] - group_pos[:, :, None]).astype(jnp.float32)
    scores = scores * score_scale + slopes[None, :, None, None] * distance[:, None, :, :]
    is_live = (key_pos[None, :] < prompt_len[:, None])[:, None, None, :]
    block_top = jnp.max(jnp.where(is_live, scores, NEG_FILL), -1)
    weights = jnp.where(is_live, jnp.exp(scores - block_top[..., None]), 0.0)
    block_sum = jnp.sum(weights, -1)
    block_acc = jnp.einsum(
        "ghqp,gphd->gqhd",
        weights.astype(jnp.bfloat16),
        val_slab,
        preferred_element_type=jnp.float32,
    )
    prompt_top = (
        jnp.transpose(block_top, (0, 2, 1))
        .reshape(requests, NEW, local_heads)[inverse]
        .reshape(row_count, local_heads)
    )
    prompt_sum = (
        jnp.transpose(block_sum, (0, 2, 1))
        .reshape(requests, NEW, local_heads)[inverse]
        .reshape(row_count, local_heads)
    )
    prompt_acc = block_acc.reshape(requests, NEW, local_heads, HD)[inverse].reshape(
        row_count, local_heads, HD
    )
    packed = jnp.concatenate(
        [prompt_acc.reshape(row_count, feat_width), prompt_top, prompt_sum], -1
    )
    (packed,) = rs_two_link(
        (to_blocks(packed, n_seq),), seq_layout, halve_order, "seq", n_seq, seq_index,
        packed_merge(feat_width, local_heads),
    )
    own_prompt = (
        packed[:, feat_width : feat_width + local_heads],
        packed[:, feat_width + local_heads :],
        packed[:, :feat_width].reshape(home_rows, local_heads, HD),
    )
    home_query = own_qkv[:, :feat_width].reshape(home_requests, NEW, local_heads, HD)
    home_pos = lax.dynamic_slice_in_dim(query_pos, seq_index * home_requests, home_requests, 0)
    home_prompt = lax.dynamic_slice_in_dim(req_prompt, seq_index * home_requests, home_requests, 0)
    home_filled = lax.dynamic_slice_in_dim(cont_len, seq_index * home_requests, home_requests, 0)
    cache_keys = cont_key.reshape(home_requests, slots, local_heads, HD)
    cache_vals = cont_val.reshape(home_requests, slots, local_heads, HD)
    slot_index = jnp.arange(slots, dtype=jnp.int32)
    cache_pos = home_prompt[:, None] + slot_index[None, :]
    cache_scores = (
        jnp.einsum("rjhd,rkhd->rhjk", home_query, cache_keys, preferred_element_type=jnp.float32)
        * score_scale
    )
    cache_scores = cache_scores + slopes[None, :, None, None] * (
        cache_pos[:, None, None, :] - home_pos[:, None, :, None]
    ).astype(jnp.float32)
    cache_live = (slot_index[None, :] < home_filled[:, None])[:, None, None, :]
    fresh_keys = key_new.reshape(home_requests, NEW, local_heads, HD)
    fresh_vals = val_new.reshape(home_requests, NEW, local_heads, HD)
    steps_new = jnp.arange(NEW, dtype=jnp.int32)
    fresh_dist = (steps_new[None, :] - steps_new[:, None]).astype(jnp.float32)
    fresh_scores = (
        jnp.einsum("rjhd,rkhd->rhjk", home_query, fresh_keys, preferred_element_type=jnp.float32)
        * score_scale
    )
    fresh_scores = fresh_scores + slopes[None, :, None, None] * fresh_dist[None, None, :, :]
    fresh_live = (steps_new[None, :] <= steps_new[:, None])[None, None, :, :]
    home_top = jnp.maximum(
        jnp.max(jnp.where(cache_live, cache_scores, NEG_FILL), -1),
        jnp.max(jnp.where(fresh_live, fresh_scores, NEG_FILL), -1),
    )
    cache_weights = jnp.where(cache_live, jnp.exp(cache_scores - home_top[..., None]), 0.0)
    fresh_weights = jnp.where(fresh_live, jnp.exp(fresh_scores - home_top[..., None]), 0.0)
    home_sum = jnp.sum(cache_weights, -1) + jnp.sum(fresh_weights, -1)
    home_acc = jnp.einsum(
        "rhjk,rkhd->rjhd",
        cache_weights.astype(jnp.bfloat16),
        cache_vals,
        preferred_element_type=jnp.float32,
    )
    home_acc = home_acc + jnp.einsum(
        "rhjk,rkhd->rjhd",
        fresh_weights.astype(jnp.bfloat16),
        fresh_vals,
        preferred_element_type=jnp.float32,
    )
    home_top = jnp.transpose(home_top, (0, 2, 1)).reshape(home_rows, local_heads)
    home_sum = jnp.transpose(home_sum, (0, 2, 1)).reshape(home_rows, local_heads)
    home_acc = home_acc.reshape(home_rows, local_heads, HD)
    merged = combine_parts(own_prompt, (home_top, home_sum, home_acc))
    own_attended = (
        (merged[2] / merged[1][..., None]).reshape(home_rows, feat_width).astype(jnp.bfloat16)
    )
    attended = ag_doubling(own_attended, "seq", n_seq, double_order, seq_index)
    attn_sum = ar_doubling(
        jnp.dot(attended, w_out, preferred_element_type=jnp.float32), "tp", n_tp, tp_bits
    )
    hidden_state = token_float + attn_sum
    second_stats = ar_doubling(
        jnp.stack([jnp.sum(hidden_state, 1), jnp.sum(hidden_state * hidden_state, 1)]),
        "seq", n_seq, halve_order,
    )
    second_normed = finish_norm(hidden_state, second_stats[0], second_stats[1], ln_second_gain)
    halves = w_up.shape[1] // 2
    up_part = jnp.einsum(
        "rk,kcn->crn",
        second_normed,
        w_up.reshape(w_up.shape[0], 2, halves),
        preferred_element_type=jnp.float32,
    )
    own_up = rs_tiled(up_part, "seq", n_seq, halve_order, seq_index)
    own_activated = jax.nn.gelu(own_up, approximate=False).astype(jnp.bfloat16)
    activated = ag_tiled(own_activated, "seq", n_seq, double_order, seq_index, row_count, halves)
    down_part = jnp.einsum(
        "crn,cnf->rf",
        activated,
        w_down.reshape(2, halves, w_down.shape[1]),
        preferred_element_type=jnp.float32,
    )
    down_sum = ar_doubling(down_part, "tp", n_tp, tp_bits)
    return (hidden_state + down_sum).astype(jnp.bfloat16)


def solution(mesh):
    in_specs = (
        P(None, "seq"),
        P("seq"),
        P("seq", None, "tp"),
        P("tp", "seq"),
        P("seq"),
        P("seq", "tp"),
        P("tp", "seq"),
        P(None, "seq", "tp"),
        P(None, "seq", "tp"),
        P("seq", None, "tp"),
        P("seq", None, "tp"),
        P(),
        P(),
        P(),
    )
    out_specs = P(None, "seq")
    return jax.shard_map(body, mesh=mesh, in_specs=in_specs, out_specs=out_specs, check_vma=False)
```

```python
import math

import jax
import jax.numpy as jnp
from jax import lax
from jax.sharding import PartitionSpec as P

D = 4096
HEADS = 32
HD = 128
NEW = 4


NEG_FILL = -1e30
NORM_EPS = 1e-05


def finish_norm(values, row_sum, row_square, gain):
    mean_row = row_sum / D
    variance = row_square / D - mean_row * mean_row
    scaled = (values - mean_row[:, None]) * lax.rsqrt(variance + NORM_EPS)[:, None]
    return (scaled * gain.astype(jnp.float32)[None, :]).astype(jnp.bfloat16)


def combine_parts(earlier, later):
    merged_top = jnp.maximum(earlier[0], later[0])
    left_factor = jnp.exp(earlier[0] - merged_top)
    right_factor = jnp.exp(later[0] - merged_top)
    merged_sum = earlier[1] * left_factor + later[1] * right_factor
    merged_acc = earlier[2] * left_factor[..., None] + later[2] * right_factor[..., None]
    return (merged_top, merged_sum, merged_acc)


def _levels(n):
    return n.bit_length() - 1


def _pairs(n, bit):
    return [(i, i ^ (1 << bit)) for i in range(n)]


def ar_doubling(x, axis, n, order):
    for bit in order:
        x = x + lax.ppermute(x, axis, _pairs(n, bit))
    return x


def add_parts(keep, got):
    return tuple(a + b for a, b in zip(keep, got))


def to_blocks(p, n):
    return p.reshape((2,) * _levels(n) + (p.shape[0] // n,) + p.shape[1:])


def rs_steps(parts, remaining, bits, axis, n, index, merge):
    remaining = list(remaining)
    for bit in bits:
        ax = remaining.index(bit)
        mine = (index >> bit) & 1
        keep = tuple(lax.dynamic_index_in_dim(p, mine, ax, keepdims=False) for p in parts)
        send = tuple(lax.dynamic_index_in_dim(p, 1 - mine, ax, keepdims=False) for p in parts)
        got = lax.ppermute(send, axis, _pairs(n, bit))
        parts = merge(keep, got)
        remaining.remove(bit)
    return parts, remaining


def rs_sum(x, axis, n, order, index, split):
    remaining = list(range(_levels(n) - 1, -1, -1))
    blocks = to_blocks(x, n)
    if split:
        half = x.shape[-1] // 2
        (low,), after = rs_steps((blocks[..., :half],), remaining, order[:2], axis, n, index, add_parts)
        (high,), _ = rs_steps((blocks[..., half:],), remaining, order[1::-1], axis, n, index, add_parts)
        blocks = jnp.concatenate([low, high], -1)
        remaining, order = after, order[2:]
    (out,), _ = rs_steps((blocks,), remaining, order, axis, n, index, add_parts)
    return out


def ag_steps(x, have, bits, axis, n, index):
    have = list(have)
    for bit in bits:
        got = lax.ppermute(x, axis, _pairs(n, bit))
        first = ((index >> bit) & 1) == 0
        low = jnp.where(first, x, got)
        high = jnp.where(first, got, x)
        pos = sum(1 for b in have if b > bit)
        x = jnp.stack([low, high], axis=pos)
        have.insert(pos, bit)
    return x, have


def ag_doubling(x, axis, n, order, index, split=False):
    levels = _levels(n)
    if split:
        x, have = ag_steps(x, [], order[:-2], axis, n, index)
        half = x.shape[-1] // 2
        low, _ = ag_steps(x[..., :half], have, order[-2:], axis, n, index)
        high, _ = ag_steps(x[..., half:], have, order[-2:][::-1], axis, n, index)
        x = jnp.concatenate([low, high], -1)
    else:
        x, _ = ag_steps(x, [], order, axis, n, index)
    return x.reshape((-1,) + x.shape[levels + 1 :])


def tiled_layout(n, rows, cols):
    levels = _levels(n)
    row_bits = levels - 1
    shape = (2,) + (2,) * row_bits + (rows >> row_bits, cols)
    layout = [0] + list(range(levels - 1, 0, -1)) + ["r", "c"]
    return shape, layout


def rs_tiled(x, axis, n, order, index):
    shape, layout = tiled_layout(n, x.shape[1], x.shape[2])
    blocks = x.reshape(shape)
    top_bit = _levels(n) - 1
    cut = layout.index(top_bit)
    low = lax.slice_in_dim(blocks, 0, 1, axis=cut)
    high = lax.slice_in_dim(blocks, 1, 2, axis=cut)
    (low,), after = rs_steps((low,), layout, order[:2], axis, n, index, add_parts)
    (high,), _ = rs_steps((high,), layout, order[1::-1], axis, n, index, add_parts)
    joined = jnp.concatenate([low, high], after.index(top_bit))
    (out,), _ = rs_steps((joined,), after, order[2:], axis, n, index, add_parts)
    return out


def ag_place(x, have, bits, layout, axis, n, index):
    have = list(have)
    for bit in bits:
        got = lax.ppermute(x, axis, _pairs(n, bit))
        first = ((index >> bit) & 1) == 0
        low = jnp.where(first, x, got)
        high = jnp.where(first, got, x)
        rank = layout.index(bit)
        pos = sum(1 for b in have if layout.index(b) < rank)
        x = jnp.stack([low, high], axis=pos)
        have.insert(pos, bit)
    return x, have


def ag_tiled(x, axis, n, order, index, rows, cols):
    shape, layout = tiled_layout(n, rows, cols)
    top_bit = _levels(n) - 1
    x, have = ag_place(x, ["r", "c"], order[:-2], layout, axis, n, index)
    cut = have.index(top_bit)
    low, done = ag_place(
        lax.slice_in_dim(x, 0, 1, axis=cut), have, order[-2:], layout, axis, n, index
    )
    high, _ = ag_place(
        lax.slice_in_dim(x, 1, 2, axis=cut), have, order[-2:][::-1], layout, axis, n, index
    )
    joined = jnp.concatenate([low, high], done.index(top_bit))
    return joined.reshape(2, rows, cols)


def rs_two_link(blocks, layout, order, axis, n, index, merge):
    top_bit = _levels(n) - 1
    cut = layout.index(top_bit)
    low = tuple(lax.slice_in_dim(p, 0, 1, axis=cut) for p in blocks)
    high = tuple(lax.slice_in_dim(p, 1, 2, axis=cut) for p in blocks)
    low, after = rs_steps(low, layout, order[:2], axis, n, index, merge)
    high, _ = rs_steps(high, layout, order[1::-1], axis, n, index, merge)
    at = after.index(top_bit)
    joined = tuple(jnp.concatenate([a, b], at) for a, b in zip(low, high))
    out, _ = rs_steps(joined, after, order[2:], axis, n, index, merge)
    return out


def stable_ranks(keys):
    count = keys.shape[0]
    order = jnp.arange(count, dtype=jnp.int32)
    before = (keys[None, :] < keys[:, None]) | (
        (keys[None, :] == keys[:, None]) & (order[None, :] < order[:, None])
    )
    rank = jnp.sum(before.astype(jnp.int32), 1)
    placed = jnp.sum(jnp.where(rank[None, :] == order[:, None], order[None, :], 0), 1)
    return placed, rank


def packed_merge(width, heads):
    def merge(keep, got):
        (mine,), (other,) = keep, got
        top = jnp.maximum(mine[..., width : width + heads], other[..., width : width + heads])
        mine_f = jnp.exp(mine[..., width : width + heads] - top)
        other_f = jnp.exp(other[..., width : width + heads] - top)
        total = mine[..., width + heads :] * mine_f + other[..., width + heads :] * other_f
        shape = mine.shape[:-1] + (heads, width // heads)
        acc = (
            mine[..., :width].reshape(shape) * mine_f[..., None]
            + other[..., :width].reshape(shape) * other_f[..., None]
        ).reshape(mine.shape[:-1] + (width,))
        return (jnp.concatenate([acc, top, total], -1),)

    return merge


def seq_orders(n):
    levels = _levels(n)
    near = [b for b in (0, 2, 1, 3, 4) if b < levels] + list(range(5, levels))
    return near, near[::-1]


def tp_order(n):
    return list(range(_levels(n)))


def body(
    tokens,
    ln_first_gain,
    w_qkv,
    w_out,
    ln_second_gain,
    w_up,
    w_down,
    prompt_key,
    prompt_val,
    cont_key,
    cont_val,
    group_ids,
    prompt_len,
    cont_len,
):
    row_count = tokens.shape[0]
    seq_index = lax.axis_index("seq")
    tp_index = lax.axis_index("tp")
    n_seq = lax.axis_size("seq")
    n_tp = lax.axis_size("tp")
    halve_order, double_order = seq_orders(n_seq)
    tp_bits = tp_order(n_tp)
    feat_width = w_qkv.shape[2]
    local_heads = feat_width // HD
    home_requests = cont_key.shape[0]
    home_rows = home_requests * NEW
    requests = row_count // NEW
    groups = prompt_key.shape[0]
    block_len = prompt_key.shape[1]
    slots = cont_key.shape[1]
    score_scale = 1.0 / math.sqrt(HD)
    token_float = tokens.astype(jnp.float32)
    first_stats = ar_doubling(
        jnp.stack([jnp.sum(token_float, 1), jnp.sum(token_float * token_float, 1)]),
        "seq", n_seq, halve_order,
    )
    normed = finish_norm(token_float, first_stats[0], first_stats[1], ln_first_gain)
    w_flat = w_qkv.reshape(w_qkv.shape[0], 3 * feat_width)
    partial_qkv = jnp.dot(normed, w_flat, preferred_element_type=jnp.float32)
    seq_layout = list(range(_levels(n_seq) - 1, -1, -1)) + ["r", "c"]
    (own_qkv,) = rs_two_link(
        (to_blocks(partial_qkv, n_seq),), seq_layout, halve_order, "seq", n_seq, seq_index, add_parts
    )
    own_qkv = own_qkv.astype(jnp.bfloat16)
    query = ag_doubling(own_qkv[:, :feat_width], "seq", n_seq, double_order, seq_index)
    key_new = own_qkv[:, feat_width : 2 * feat_width]
    val_new = own_qkv[:, 2 * feat_width :]
    head_first = (tp_index * local_heads).astype(jnp.float32)
    slopes = jnp.exp2(
        -8.0 * (head_first + jnp.arange(local_heads, dtype=jnp.float32) + 1.0) / HEADS
    )
    placed, inverse = stable_ranks(group_ids)
    members = placed.reshape(groups, requests // groups)
    group_match = group_ids[:, None] == jnp.arange(groups, dtype=jnp.int32)[None, :]
    req_prompt = jnp.sum(jnp.where(group_match, prompt_len[None, :], 0), 1)
    query_pos = (req_prompt + cont_len)[:, None] + jnp.arange(NEW, dtype=jnp.int32)[None, :]
    query_req = query.reshape(requests, NEW, local_heads, HD)
    group_query = query_req[members].reshape(groups, -1, local_heads, HD)
    group_pos = query_pos[members].reshape(groups, -1)
    key_slab = prompt_key.reshape(groups, block_len, local_heads, HD)
    val_slab = prompt_val.reshape(groups, block_len, local_heads, HD)
    key_pos = seq_index * block_len + jnp.arange(block_len, dtype=jnp.int32)
    scores = jnp.einsum(
        "gqhd,gphd->ghqp", group_query, key_slab, preferred_element_type=jnp.float32
    )
    distance = (key_pos[None, None, :] - group_pos[:, :, None]).astype(jnp.float32)
    scores = scores * score_scale + slopes[None, :, None, None] * distance[:, None, :, :]
    is_live = (key_pos[None, :] < prompt_len[:, None])[:, None, None, :]
    block_top = jnp.max(jnp.where(is_live, scores, NEG_FILL), -1)
    weights = jnp.where(is_live, jnp.exp(scores - block_top[..., None]), 0.0)
    block_sum = jnp.sum(weights, -1)
    block_acc = jnp.einsum(
        "ghqp,gphd->gqhd",
        weights.astype(jnp.bfloat16),
        val_slab,
        preferred_element_type=jnp.float32,
    )
    prompt_top = (
        jnp.transpose(block_top, (0, 2, 1))
        .reshape(requests, NEW, local_heads)[inverse]
        .reshape(row_count, local_heads)
    )
    prompt_sum = (
        jnp.transpose(block_sum, (0, 2, 1))
        .reshape(requests, NEW, local_heads)[inverse]
        .reshape(row_count, local_heads)
    )
    prompt_acc = block_acc.reshape(requests, NEW, local_heads, HD)[inverse].reshape(
        row_count, local_heads, HD
    )
    home_query = own_qkv[:, :feat_width].reshape(home_requests, NEW, local_heads, HD)
    home_pos = lax.dynamic_slice_in_dim(query_pos, seq_index * home_requests, home_requests, 0)
    home_prompt = lax.dynamic_slice_in_dim(req_prompt, seq_index * home_requests, home_requests, 0)
    home_filled = lax.dynamic_slice_in_dim(cont_len, seq_index * home_requests, home_requests, 0)
    cache_keys = cont_key.reshape(home_requests, slots, local_heads, HD)
    cache_vals = cont_val.reshape(home_requests, slots, local_heads, HD)
    slot_index = jnp.arange(slots, dtype=jnp.int32)
    cache_pos = home_prompt[:, None] + slot_index[None, :]
    cache_scores = (
        jnp.einsum("rjhd,rkhd->rhjk", home_query, cache_keys, preferred_element_type=jnp.float32)
        * score_scale
    )
    cache_scores = cache_scores + slopes[None, :, None, None] * (
        cache_pos[:, None, None, :] - home_pos[:, None, :, None]
    ).astype(jnp.float32)
    cache_live = (slot_index[None, :] < home_filled[:, None])[:, None, None, :]
    fresh_keys = key_new.reshape(home_requests, NEW, local_heads, HD)
    fresh_vals = val_new.reshape(home_requests, NEW, local_heads, HD)
    steps_new = jnp.arange(NEW, dtype=jnp.int32)
    fresh_dist = (steps_new[None, :] - steps_new[:, None]).astype(jnp.float32)
    fresh_scores = (
        jnp.einsum("rjhd,rkhd->rhjk", home_query, fresh_keys, preferred_element_type=jnp.float32)
        * score_scale
    )
    fresh_scores = fresh_scores + slopes[None, :, None, None] * fresh_dist[None, None, :, :]
    fresh_live = (steps_new[None, :] <= steps_new[:, None])[None, None, :, :]
    home_top = jnp.maximum(
        jnp.max(jnp.where(cache_live, cache_scores, NEG_FILL), -1),
        jnp.max(jnp.where(fresh_live, fresh_scores, NEG_FILL), -1),
    )
    cache_weights = jnp.where(cache_live, jnp.exp(cache_scores - home_top[..., None]), 0.0)
    fresh_weights = jnp.where(fresh_live, jnp.exp(fresh_scores - home_top[..., None]), 0.0)
    home_sum = jnp.sum(cache_weights, -1) + jnp.sum(fresh_weights, -1)
    home_acc = jnp.einsum(
        "rhjk,rkhd->rjhd",
        cache_weights.astype(jnp.bfloat16),
        cache_vals,
        preferred_element_type=jnp.float32,
    )
    home_acc = home_acc + jnp.einsum(
        "rhjk,rkhd->rjhd",
        fresh_weights.astype(jnp.bfloat16),
        fresh_vals,
        preferred_element_type=jnp.float32,
    )
    home_top = jnp.transpose(home_top, (0, 2, 1)).reshape(home_rows, local_heads)
    home_sum = jnp.transpose(home_sum, (0, 2, 1)).reshape(home_rows, local_heads)
    home_acc = home_acc.reshape(home_rows, local_heads, HD)
    merge = packed_merge(feat_width, local_heads)
    packed = jnp.concatenate(
        [prompt_acc.reshape(row_count, feat_width), prompt_top, prompt_sum], -1
    )
    home_packed = jnp.concatenate([home_acc.reshape(home_rows, feat_width), home_top, home_sum], -1)
    row_start = seq_index * home_rows
    (own_rows,) = merge((lax.dynamic_slice_in_dim(packed, row_start, home_rows, 0),), (home_packed,))
    packed = lax.dynamic_update_slice_in_dim(packed, own_rows, row_start, 0)
    near_bits = halve_order[:2]
    far_bits = halve_order[2:]
    (packed,) = rs_two_link(
        (to_blocks(packed, n_seq),), seq_layout, near_bits, "seq", n_seq, seq_index, merge
    )
    for bit in far_bits:
        (packed,) = merge((packed,), (lax.ppermute(packed, "seq", _pairs(n_seq, bit)),))
    part_attended = (
        packed[..., :feat_width].reshape(packed.shape[:-1] + (local_heads, HD))
        / packed[..., feat_width + local_heads :][..., None]
    ).reshape(packed.shape[:-1] + (feat_width,)).astype(jnp.bfloat16)
    near_have = [b for b in seq_layout if b not in near_bits]
    attended, _ = ag_place(
        part_attended, near_have, near_bits[::-1], seq_layout, "seq", n_seq, seq_index
    )
    attended = attended.reshape(row_count, feat_width)
    attn_sum = ar_doubling(
        jnp.dot(attended, w_out, preferred_element_type=jnp.float32), "tp", n_tp, tp_bits
    )
    hidden_state = token_float + attn_sum
    second_stats = ar_doubling(
        jnp.stack([jnp.sum(hidden_state, 1), jnp.sum(hidden_state * hidden_state, 1)]),
        "seq", n_seq, halve_order,
    )
    second_normed = finish_norm(hidden_state, second_stats[0], second_stats[1], ln_second_gain)
    halves = w_up.shape[1] // 2
    up_part = jnp.einsum(
        "rk,kcn->crn",
        second_normed,
        w_up.reshape(w_up.shape[0], 2, halves),
        preferred_element_type=jnp.float32,
    )
    own_up = rs_tiled(up_part, "seq", n_seq, halve_order, seq_index)
    own_activated = jax.nn.gelu(own_up, approximate=False).astype(jnp.bfloat16)
    activated = ag_tiled(own_activated, "seq", n_seq, double_order, seq_index, row_count, halves)
    down_part = jnp.einsum(
        "crn,cnf->rf",
        activated,
        w_down.reshape(2, halves, w_down.shape[1]),
        preferred_element_type=jnp.float32,
    )
    down_sum = ar_doubling(down_part, "tp", n_tp, tp_bits)
    return (hidden_state + down_sum).astype(jnp.bfloat16)


def solution(mesh):
    in_specs = (
        P(None, "seq"),
        P("seq"),
        P("seq", None, "tp"),
        P("tp", "seq"),
        P("seq"),
        P("seq", "tp"),
        P("tp", "seq"),
        P(None, "seq", "tp"),
        P(None, "seq", "tp"),
        P("seq", None, "tp"),
        P("seq", None, "tp"),
        P(),
        P(),
        P(),
    )
    out_specs = P(None, "seq")
    return jax.shard_map(body, mesh=mesh, in_specs=in_specs, out_specs=out_specs, check_vma=False)
```

```python
import math

import jax
import jax.numpy as jnp
from jax import lax
from jax.sharding import PartitionSpec as P

D = 4096
HEADS = 32
HD = 128
NEW = 4


NEG_FILL = -1e30
NORM_EPS = 1e-05


def finish_norm(values, row_sum, row_square, gain):
    mean_row = row_sum / D
    variance = row_square / D - mean_row * mean_row
    scaled = (values - mean_row[:, None]) * lax.rsqrt(variance + NORM_EPS)[:, None]
    return (scaled * gain.astype(jnp.float32)[None, :]).astype(jnp.bfloat16)


def combine_parts(earlier, later):
    merged_top = jnp.maximum(earlier[0], later[0])
    left_factor = jnp.exp(earlier[0] - merged_top)
    right_factor = jnp.exp(later[0] - merged_top)
    merged_sum = earlier[1] * left_factor + later[1] * right_factor
    merged_acc = earlier[2] * left_factor[..., None] + later[2] * right_factor[..., None]
    return (merged_top, merged_sum, merged_acc)


def _levels(n):
    return n.bit_length() - 1


def _pairs(n, bit):
    return [(i, i ^ (1 << bit)) for i in range(n)]


def ar_doubling(x, axis, n, order):
    for bit in order:
        x = x + lax.ppermute(x, axis, _pairs(n, bit))
    return x


def add_parts(keep, got):
    return tuple(a + b for a, b in zip(keep, got))


def to_blocks(p, n):
    return p.reshape((2,) * _levels(n) + (p.shape[0] // n,) + p.shape[1:])


def rs_steps(parts, remaining, bits, axis, n, index, merge):
    remaining = list(remaining)
    for bit in bits:
        ax = remaining.index(bit)
        mine = (index >> bit) & 1
        keep = tuple(lax.dynamic_index_in_dim(p, mine, ax, keepdims=False) for p in parts)
        send = tuple(lax.dynamic_index_in_dim(p, 1 - mine, ax, keepdims=False) for p in parts)
        got = lax.ppermute(send, axis, _pairs(n, bit))
        parts = merge(keep, got)
        remaining.remove(bit)
    return parts, remaining


def rs_sum(x, axis, n, order, index, split):
    remaining = list(range(_levels(n) - 1, -1, -1))
    blocks = to_blocks(x, n)
    if split:
        half = x.shape[-1] // 2
        (low,), after = rs_steps((blocks[..., :half],), remaining, order[:2], axis, n, index, add_parts)
        (high,), _ = rs_steps((blocks[..., half:],), remaining, order[1::-1], axis, n, index, add_parts)
        blocks = jnp.concatenate([low, high], -1)
        remaining, order = after, order[2:]
    (out,), _ = rs_steps((blocks,), remaining, order, axis, n, index, add_parts)
    return out


def ag_steps(x, have, bits, axis, n, index):
    have = list(have)
    for bit in bits:
        got = lax.ppermute(x, axis, _pairs(n, bit))
        first = ((index >> bit) & 1) == 0
        low = jnp.where(first, x, got)
        high = jnp.where(first, got, x)
        pos = sum(1 for b in have if b > bit)
        x = jnp.stack([low, high], axis=pos)
        have.insert(pos, bit)
    return x, have


def ag_doubling(x, axis, n, order, index, split=False):
    levels = _levels(n)
    if split:
        x, have = ag_steps(x, [], order[:-2], axis, n, index)
        half = x.shape[-1] // 2
        low, _ = ag_steps(x[..., :half], have, order[-2:], axis, n, index)
        high, _ = ag_steps(x[..., half:], have, order[-2:][::-1], axis, n, index)
        x = jnp.concatenate([low, high], -1)
    else:
        x, _ = ag_steps(x, [], order, axis, n, index)
    return x.reshape((-1,) + x.shape[levels + 1 :])


def tiled_layout(n, rows, cols):
    levels = _levels(n)
    row_bits = levels - 1
    shape = (2,) + (2,) * row_bits + (rows >> row_bits, cols)
    layout = [0] + list(range(levels - 1, 0, -1)) + ["r", "c"]
    return shape, layout


def rs_tiled(x, axis, n, order, index):
    shape, layout = tiled_layout(n, x.shape[1], x.shape[2])
    blocks = x.reshape(shape)
    top_bit = _levels(n) - 1
    cut = layout.index(top_bit)
    low = lax.slice_in_dim(blocks, 0, 1, axis=cut)
    high = lax.slice_in_dim(blocks, 1, 2, axis=cut)
    (low,), after = rs_steps((low,), layout, order[:2], axis, n, index, add_parts)
    (high,), _ = rs_steps((high,), layout, order[1::-1], axis, n, index, add_parts)
    joined = jnp.concatenate([low, high], after.index(top_bit))
    (out,), _ = rs_steps((joined,), after, order[2:], axis, n, index, add_parts)
    return out


def ag_place(x, have, bits, layout, axis, n, index):
    have = list(have)
    for bit in bits:
        got = lax.ppermute(x, axis, _pairs(n, bit))
        first = ((index >> bit) & 1) == 0
        low = jnp.where(first, x, got)
        high = jnp.where(first, got, x)
        rank = layout.index(bit)
        pos = sum(1 for b in have if layout.index(b) < rank)
        x = jnp.stack([low, high], axis=pos)
        have.insert(pos, bit)
    return x, have


def ag_tiled(x, axis, n, order, index, rows, cols):
    shape, layout = tiled_layout(n, rows, cols)
    top_bit = _levels(n) - 1
    x, have = ag_place(x, ["r", "c"], order[:-2], layout, axis, n, index)
    cut = have.index(top_bit)
    low, done = ag_place(
        lax.slice_in_dim(x, 0, 1, axis=cut), have, order[-2:], layout, axis, n, index
    )
    high, _ = ag_place(
        lax.slice_in_dim(x, 1, 2, axis=cut), have, order[-2:][::-1], layout, axis, n, index
    )
    joined = jnp.concatenate([low, high], done.index(top_bit))
    return joined.reshape(2, rows, cols)


def rs_two_link(blocks, layout, order, axis, n, index, merge):
    top_bit = _levels(n) - 1
    cut = layout.index(top_bit)
    low = tuple(lax.slice_in_dim(p, 0, 1, axis=cut) for p in blocks)
    high = tuple(lax.slice_in_dim(p, 1, 2, axis=cut) for p in blocks)
    low, after = rs_steps(low, layout, order[:2], axis, n, index, merge)
    high, _ = rs_steps(high, layout, order[1::-1], axis, n, index, merge)
    at = after.index(top_bit)
    joined = tuple(jnp.concatenate([a, b], at) for a, b in zip(low, high))
    out, _ = rs_steps(joined, after, order[2:], axis, n, index, merge)
    return out


def stable_ranks(keys):
    count = keys.shape[0]
    order = jnp.arange(count, dtype=jnp.int32)
    before = (keys[None, :] < keys[:, None]) | (
        (keys[None, :] == keys[:, None]) & (order[None, :] < order[:, None])
    )
    rank = jnp.sum(before.astype(jnp.int32), 1)
    placed = jnp.sum(jnp.where(rank[None, :] == order[:, None], order[None, :], 0), 1)
    return placed, rank


def packed_merge(width, heads):
    def merge(keep, got):
        (mine,), (other,) = keep, got
        top = jnp.maximum(mine[..., width : width + heads], other[..., width : width + heads])
        mine_f = jnp.exp(mine[..., width : width + heads] - top)
        other_f = jnp.exp(other[..., width : width + heads] - top)
        total = mine[..., width + heads :] * mine_f + other[..., width + heads :] * other_f
        shape = mine.shape[:-1] + (heads, width // heads)
        acc = (
            mine[..., :width].reshape(shape) * mine_f[..., None]
            + other[..., :width].reshape(shape) * other_f[..., None]
        ).reshape(mine.shape[:-1] + (width,))
        return (jnp.concatenate([acc, top, total], -1),)

    return merge


def seq_orders(n):
    levels = _levels(n)
    near = [b for b in (0, 2, 1, 3, 4) if b < levels] + list(range(5, levels))
    return near, near[::-1]


def tp_order(n):
    return list(range(_levels(n)))


def body(
    tokens,
    ln_first_gain,
    w_qkv,
    w_out,
    ln_second_gain,
    w_up,
    w_down,
    prompt_key,
    prompt_val,
    cont_key,
    cont_val,
    group_ids,
    prompt_len,
    cont_len,
):
    row_count = tokens.shape[0]
    seq_index = lax.axis_index("seq")
    tp_index = lax.axis_index("tp")
    n_seq = lax.axis_size("seq")
    n_tp = lax.axis_size("tp")
    halve_order, double_order = seq_orders(n_seq)
    tp_bits = tp_order(n_tp)
    feat_width = w_qkv.shape[2]
    local_heads = feat_width // HD
    home_requests = cont_key.shape[0]
    home_rows = home_requests * NEW
    requests = row_count // NEW
    groups = prompt_key.shape[0]
    block_len = prompt_key.shape[1]
    slots = cont_key.shape[1]
    score_scale = 1.0 / math.sqrt(HD)
    token_float = tokens.astype(jnp.float32)
    first_stats = ar_doubling(
        jnp.stack([jnp.sum(token_float, 1), jnp.sum(token_float * token_float, 1)]),
        "seq", n_seq, halve_order,
    )
    normed = finish_norm(token_float, first_stats[0], first_stats[1], ln_first_gain)
    w_flat = w_qkv.reshape(w_qkv.shape[0], 3 * feat_width)
    partial_qkv = jnp.dot(normed, w_flat, preferred_element_type=jnp.float32)
    seq_layout = list(range(_levels(n_seq) - 1, -1, -1)) + ["r", "c"]
    (own_qkv,) = rs_two_link(
        (to_blocks(partial_qkv, n_seq),), seq_layout, halve_order, "seq", n_seq, seq_index, add_parts
    )
    own_qkv = own_qkv.astype(jnp.bfloat16)
    query = ag_doubling(own_qkv[:, :feat_width], "seq", n_seq, double_order, seq_index)
    key_new = own_qkv[:, feat_width : 2 * feat_width]
    val_new = own_qkv[:, 2 * feat_width :]
    head_first = (tp_index * local_heads).astype(jnp.float32)
    slopes = jnp.exp2(
        -8.0 * (head_first + jnp.arange(local_heads, dtype=jnp.float32) + 1.0) / HEADS
    )
    placed, inverse = stable_ranks(group_ids)
    members = placed.reshape(groups, requests // groups)
    group_match = group_ids[:, None] == jnp.arange(groups, dtype=jnp.int32)[None, :]
    req_prompt = jnp.sum(jnp.where(group_match, prompt_len[None, :], 0), 1)
    query_pos = (req_prompt + cont_len)[:, None] + jnp.arange(NEW, dtype=jnp.int32)[None, :]
    query_req = query.reshape(requests, NEW, local_heads, HD)
    group_query = query_req[members].reshape(groups, -1, local_heads, HD)
    group_pos = query_pos[members].reshape(groups, -1)
    key_slab = prompt_key.reshape(groups, block_len, local_heads, HD)
    val_slab = prompt_val.reshape(groups, block_len, local_heads, HD)
    key_pos = seq_index * block_len + jnp.arange(block_len, dtype=jnp.int32)
    scores = jnp.einsum(
        "gqhd,gphd->ghqp", group_query, key_slab, preferred_element_type=jnp.float32
    )
    distance = (key_pos[None, None, :] - group_pos[:, :, None]).astype(jnp.float32)
    scores = scores * score_scale + slopes[None, :, None, None] * distance[:, None, :, :]
    is_live = (key_pos[None, :] < prompt_len[:, None])[:, None, None, :]
    block_top = jnp.max(jnp.where(is_live, scores, NEG_FILL), -1)
    weights = jnp.where(is_live, jnp.exp(scores - block_top[..., None]), 0.0)
    block_sum = jnp.sum(weights, -1)
    block_acc = jnp.einsum(
        "ghqp,gphd->gqhd",
        weights.astype(jnp.bfloat16),
        val_slab,
        preferred_element_type=jnp.float32,
    )
    prompt_top = (
        jnp.transpose(block_top, (0, 2, 1))
        .reshape(requests, NEW, local_heads)[inverse]
        .reshape(row_count, local_heads)
    )
    prompt_sum = (
        jnp.transpose(block_sum, (0, 2, 1))
        .reshape(requests, NEW, local_heads)[inverse]
        .reshape(row_count, local_heads)
    )
    prompt_acc = block_acc.reshape(requests, NEW, local_heads, HD)[inverse].reshape(
        row_count, local_heads, HD
    )
    home_query = own_qkv[:, :feat_width].reshape(home_requests, NEW, local_heads, HD)
    home_pos = lax.dynamic_slice_in_dim(query_pos, seq_index * home_requests, home_requests, 0)
    home_prompt = lax.dynamic_slice_in_dim(req_prompt, seq_index * home_requests, home_requests, 0)
    home_filled = lax.dynamic_slice_in_dim(cont_len, seq_index * home_requests, home_requests, 0)
    cache_keys = cont_key.reshape(home_requests, slots, local_heads, HD)
    cache_vals = cont_val.reshape(home_requests, slots, local_heads, HD)
    slot_index = jnp.arange(slots, dtype=jnp.int32)
    cache_pos = home_prompt[:, None] + slot_index[None, :]
    cache_scores = (
        jnp.einsum("rjhd,rkhd->rhjk", home_query, cache_keys, preferred_element_type=jnp.float32)
        * score_scale
    )
    cache_scores = cache_scores + slopes[None, :, None, None] * (
        cache_pos[:, None, None, :] - home_pos[:, None, :, None]
    ).astype(jnp.float32)
    cache_live = (slot_index[None, :] < home_filled[:, None])[:, None, None, :]
    fresh_keys = key_new.reshape(home_requests, NEW, local_heads, HD)
    fresh_vals = val_new.reshape(home_requests, NEW, local_heads, HD)
    steps_new = jnp.arange(NEW, dtype=jnp.int32)
    fresh_dist = (steps_new[None, :] - steps_new[:, None]).astype(jnp.float32)
    fresh_scores = (
        jnp.einsum("rjhd,rkhd->rhjk", home_query, fresh_keys, preferred_element_type=jnp.float32)
        * score_scale
    )
    fresh_scores = fresh_scores + slopes[None, :, None, None] * fresh_dist[None, None, :, :]
    fresh_live = (steps_new[None, :] <= steps_new[:, None])[None, None, :, :]
    home_top = jnp.maximum(
        jnp.max(jnp.where(cache_live, cache_scores, NEG_FILL), -1),
        jnp.max(jnp.where(fresh_live, fresh_scores, NEG_FILL), -1),
    )
    cache_weights = jnp.where(cache_live, jnp.exp(cache_scores - home_top[..., None]), 0.0)
    fresh_weights = jnp.where(fresh_live, jnp.exp(fresh_scores - home_top[..., None]), 0.0)
    home_sum = jnp.sum(cache_weights, -1) + jnp.sum(fresh_weights, -1)
    home_acc = jnp.einsum(
        "rhjk,rkhd->rjhd",
        cache_weights.astype(jnp.bfloat16),
        cache_vals,
        preferred_element_type=jnp.float32,
    )
    home_acc = home_acc + jnp.einsum(
        "rhjk,rkhd->rjhd",
        fresh_weights.astype(jnp.bfloat16),
        fresh_vals,
        preferred_element_type=jnp.float32,
    )
    home_top = jnp.transpose(home_top, (0, 2, 1)).reshape(home_rows, local_heads)
    home_sum = jnp.transpose(home_sum, (0, 2, 1)).reshape(home_rows, local_heads)
    home_acc = home_acc.reshape(home_rows, local_heads, HD)
    merge = packed_merge(feat_width, local_heads)
    packed = jnp.concatenate(
        [prompt_acc.reshape(row_count, feat_width), prompt_top, prompt_sum], -1
    )
    home_packed = jnp.concatenate([home_acc.reshape(home_rows, feat_width), home_top, home_sum], -1)
    near_bits = halve_order[:2]
    far_bits = halve_order[2:]
    (packed,) = rs_two_link(
        (to_blocks(packed, n_seq),), seq_layout, near_bits, "seq", n_seq, seq_index, merge
    )
    near_have = [b for b in seq_layout if b not in near_bits]
    corner = [(seq_index >> b) & 1 for b in near_have if b not in ("r", "c")] + [0, 0]
    one_block = (1,) * len(far_bits) + home_packed.shape
    own_block = lax.dynamic_slice(packed, corner, one_block).reshape(home_packed.shape)
    (own_block,) = merge((own_block,), (home_packed,))
    packed = lax.dynamic_update_slice(packed, own_block.reshape(one_block), corner)
    for bit in far_bits:
        (packed,) = merge((packed,), (lax.ppermute(packed, "seq", _pairs(n_seq, bit)),))
    part_attended = (
        packed[..., :feat_width].reshape(packed.shape[:-1] + (local_heads, HD))
        / packed[..., feat_width + local_heads :][..., None]
    ).reshape(packed.shape[:-1] + (feat_width,)).astype(jnp.bfloat16)
    attended, _ = ag_place(
        part_attended, near_have, near_bits[::-1], seq_layout, "seq", n_seq, seq_index
    )
    attended = attended.reshape(row_count, feat_width)
    attn_sum = ar_doubling(
        jnp.dot(attended, w_out, preferred_element_type=jnp.float32), "tp", n_tp, tp_bits
    )
    hidden_state = token_float + attn_sum
    second_stats = ar_doubling(
        jnp.stack([jnp.sum(hidden_state, 1), jnp.sum(hidden_state * hidden_state, 1)]),
        "seq", n_seq, halve_order,
    )
    second_normed = finish_norm(hidden_state, second_stats[0], second_stats[1], ln_second_gain)
    halves = w_up.shape[1] // 2
    up_part = jnp.einsum(
        "rk,kcn->crn",
        second_normed,
        w_up.reshape(w_up.shape[0], 2, halves),
        preferred_element_type=jnp.float32,
    )
    own_up = rs_tiled(up_part, "seq", n_seq, halve_order, seq_index)
    own_activated = jax.nn.gelu(own_up, approximate=False).astype(jnp.bfloat16)
    activated = ag_tiled(own_activated, "seq", n_seq, double_order, seq_index, row_count, halves)
    down_part = jnp.einsum(
        "crn,cnf->rf",
        activated,
        w_down.reshape(2, halves, w_down.shape[1]),
        preferred_element_type=jnp.float32,
    )
    down_sum = ar_doubling(down_part, "tp", n_tp, tp_bits)
    return (hidden_state + down_sum).astype(jnp.bfloat16)


def solution(mesh):
    in_specs = (
        P(None, "seq"),
        P("seq"),
        P("seq", None, "tp"),
        P("tp", "seq"),
        P("seq"),
        P("seq", "tp"),
        P("tp", "seq"),
        P(None, "seq", "tp"),
        P(None, "seq", "tp"),
        P("seq", None, "tp"),
        P("seq", None, "tp"),
        P(),
        P(),
        P(),
    )
    out_specs = P(None, "seq")
    return jax.shard_map(body, mesh=mesh, in_specs=in_specs, out_specs=out_specs, check_vma=False)
```

```python
import math

import jax
import jax.numpy as jnp
from jax import lax
from jax.sharding import PartitionSpec as P

D = 4096
HEADS = 32
HD = 128
NEW = 4


NEG_FILL = -1e30
NORM_EPS = 1e-05


def finish_norm(values, row_sum, row_square, gain):
    mean_row = row_sum / D
    variance = row_square / D - mean_row * mean_row
    scaled = (values - mean_row[:, None]) * lax.rsqrt(variance + NORM_EPS)[:, None]
    return (scaled * gain.astype(jnp.float32)[None, :]).astype(jnp.bfloat16)


def combine_parts(earlier, later):
    merged_top = jnp.maximum(earlier[0], later[0])
    left_factor = jnp.exp(earlier[0] - merged_top)
    right_factor = jnp.exp(later[0] - merged_top)
    merged_sum = earlier[1] * left_factor + later[1] * right_factor
    merged_acc = earlier[2] * left_factor[..., None] + later[2] * right_factor[..., None]
    return (merged_top, merged_sum, merged_acc)


def _levels(n):
    return n.bit_length() - 1


def _pairs(n, bit):
    return [(i, i ^ (1 << bit)) for i in range(n)]


def ar_doubling(x, axis, n, order):
    for bit in order:
        x = x + lax.ppermute(x, axis, _pairs(n, bit))
    return x


def add_parts(keep, got):
    return tuple(a + b for a, b in zip(keep, got))


def to_blocks(p, n):
    return p.reshape((2,) * _levels(n) + (p.shape[0] // n,) + p.shape[1:])


def rs_steps(parts, remaining, bits, axis, n, index, merge):
    remaining = list(remaining)
    for bit in bits:
        ax = remaining.index(bit)
        mine = (index >> bit) & 1
        keep = tuple(lax.dynamic_index_in_dim(p, mine, ax, keepdims=False) for p in parts)
        send = tuple(lax.dynamic_index_in_dim(p, 1 - mine, ax, keepdims=False) for p in parts)
        got = lax.ppermute(send, axis, _pairs(n, bit))
        parts = merge(keep, got)
        remaining.remove(bit)
    return parts, remaining


def rs_sum(x, axis, n, order, index, split):
    remaining = list(range(_levels(n) - 1, -1, -1))
    blocks = to_blocks(x, n)
    if split:
        half = x.shape[-1] // 2
        (low,), after = rs_steps((blocks[..., :half],), remaining, order[:2], axis, n, index, add_parts)
        (high,), _ = rs_steps((blocks[..., half:],), remaining, order[1::-1], axis, n, index, add_parts)
        blocks = jnp.concatenate([low, high], -1)
        remaining, order = after, order[2:]
    (out,), _ = rs_steps((blocks,), remaining, order, axis, n, index, add_parts)
    return out


def ag_steps(x, have, bits, axis, n, index):
    have = list(have)
    for bit in bits:
        got = lax.ppermute(x, axis, _pairs(n, bit))
        first = ((index >> bit) & 1) == 0
        low = jnp.where(first, x, got)
        high = jnp.where(first, got, x)
        pos = sum(1 for b in have if b > bit)
        x = jnp.stack([low, high], axis=pos)
        have.insert(pos, bit)
    return x, have


def ag_doubling(x, axis, n, order, index, split=False):
    levels = _levels(n)
    if split:
        x, have = ag_steps(x, [], order[:-2], axis, n, index)
        half = x.shape[-1] // 2
        low, _ = ag_steps(x[..., :half], have, order[-2:], axis, n, index)
        high, _ = ag_steps(x[..., half:], have, order[-2:][::-1], axis, n, index)
        x = jnp.concatenate([low, high], -1)
    else:
        x, _ = ag_steps(x, [], order, axis, n, index)
    return x.reshape((-1,) + x.shape[levels + 1 :])


def tiled_layout(n, rows, cols):
    levels = _levels(n)
    row_bits = levels - 1
    shape = (2,) + (2,) * row_bits + (rows >> row_bits, cols)
    layout = [0] + list(range(levels - 1, 0, -1)) + ["r", "c"]
    return shape, layout


def rs_tiled(x, axis, n, order, index):
    shape, layout = tiled_layout(n, x.shape[1], x.shape[2])
    blocks = x.reshape(shape)
    top_bit = _levels(n) - 1
    cut = layout.index(top_bit)
    low = lax.slice_in_dim(blocks, 0, 1, axis=cut)
    high = lax.slice_in_dim(blocks, 1, 2, axis=cut)
    (low,), after = rs_steps((low,), layout, order[:2], axis, n, index, add_parts)
    (high,), _ = rs_steps((high,), layout, order[1::-1], axis, n, index, add_parts)
    joined = jnp.concatenate([low, high], after.index(top_bit))
    (out,), _ = rs_steps((joined,), after, order[2:], axis, n, index, add_parts)
    return out


def ag_place(x, have, bits, layout, axis, n, index):
    have = list(have)
    for bit in bits:
        got = lax.ppermute(x, axis, _pairs(n, bit))
        first = ((index >> bit) & 1) == 0
        low = jnp.where(first, x, got)
        high = jnp.where(first, got, x)
        rank = layout.index(bit)
        pos = sum(1 for b in have if layout.index(b) < rank)
        x = jnp.stack([low, high], axis=pos)
        have.insert(pos, bit)
    return x, have


def ag_tiled(x, axis, n, order, index, rows, cols):
    shape, layout = tiled_layout(n, rows, cols)
    top_bit = _levels(n) - 1
    x, have = ag_place(x, ["r", "c"], order[:-2], layout, axis, n, index)
    cut = have.index(top_bit)
    low, done = ag_place(
        lax.slice_in_dim(x, 0, 1, axis=cut), have, order[-2:], layout, axis, n, index
    )
    high, _ = ag_place(
        lax.slice_in_dim(x, 1, 2, axis=cut), have, order[-2:][::-1], layout, axis, n, index
    )
    joined = jnp.concatenate([low, high], done.index(top_bit))
    return joined.reshape(2, rows, cols)


def rs_two_link(blocks, layout, order, axis, n, index, merge):
    top_bit = _levels(n) - 1
    cut = layout.index(top_bit)
    low = tuple(lax.slice_in_dim(p, 0, 1, axis=cut) for p in blocks)
    high = tuple(lax.slice_in_dim(p, 1, 2, axis=cut) for p in blocks)
    low, after = rs_steps(low, layout, order[:2], axis, n, index, merge)
    high, _ = rs_steps(high, layout, order[1::-1], axis, n, index, merge)
    at = after.index(top_bit)
    joined = tuple(jnp.concatenate([a, b], at) for a, b in zip(low, high))
    out, _ = rs_steps(joined, after, order[2:], axis, n, index, merge)
    return out


def stable_ranks(keys):
    count = keys.shape[0]
    order = jnp.arange(count, dtype=jnp.int32)
    before = (keys[None, :] < keys[:, None]) | (
        (keys[None, :] == keys[:, None]) & (order[None, :] < order[:, None])
    )
    rank = jnp.sum(before.astype(jnp.int32), 1)
    placed = jnp.sum(jnp.where(rank[None, :] == order[:, None], order[None, :], 0), 1)
    return placed, rank


def packed_merge(width, heads):
    def merge(keep, got):
        (mine,), (other,) = keep, got
        top = jnp.maximum(mine[..., width : width + heads], other[..., width : width + heads])
        mine_f = jnp.exp(mine[..., width : width + heads] - top)
        other_f = jnp.exp(other[..., width : width + heads] - top)
        total = mine[..., width + heads :] * mine_f + other[..., width + heads :] * other_f
        shape = mine.shape[:-1] + (heads, width // heads)
        acc = (
            mine[..., :width].reshape(shape) * mine_f[..., None]
            + other[..., :width].reshape(shape) * other_f[..., None]
        ).reshape(mine.shape[:-1] + (width,))
        return (jnp.concatenate([acc, top, total], -1),)

    return merge


def seq_orders(n):
    levels = _levels(n)
    near = [b for b in (0, 2, 1, 3, 4) if b < levels] + list(range(5, levels))
    return near, near[::-1]


def tp_order(n):
    return list(range(_levels(n)))


def body(
    tokens,
    ln_first_gain,
    w_qkv,
    w_out,
    ln_second_gain,
    w_up,
    w_down,
    prompt_key,
    prompt_val,
    cont_key,
    cont_val,
    group_ids,
    prompt_len,
    cont_len,
):
    row_count = tokens.shape[0]
    seq_index = lax.axis_index("seq")
    tp_index = lax.axis_index("tp")
    n_seq = lax.axis_size("seq")
    n_tp = lax.axis_size("tp")
    halve_order, double_order = seq_orders(n_seq)
    tp_bits = tp_order(n_tp)
    feat_width = w_qkv.shape[2]
    local_heads = feat_width // HD
    home_requests = cont_key.shape[0]
    home_rows = home_requests * NEW
    requests = row_count // NEW
    groups = prompt_key.shape[0]
    block_len = prompt_key.shape[1]
    slots = cont_key.shape[1]
    score_scale = 1.0 / math.sqrt(HD)
    token_float = tokens.astype(jnp.float32)
    first_stats = ar_doubling(
        jnp.stack([jnp.sum(token_float, 1), jnp.sum(token_float * token_float, 1)]),
        "seq", n_seq, halve_order,
    )
    normed = finish_norm(token_float, first_stats[0], first_stats[1], ln_first_gain)
    w_flat = w_qkv.reshape(w_qkv.shape[0], 3 * feat_width)
    partial_qkv = jnp.dot(normed, w_flat, preferred_element_type=jnp.float32)
    seq_layout = list(range(_levels(n_seq) - 1, -1, -1)) + ["r", "c"]
    (own_qkv,) = rs_two_link(
        (to_blocks(partial_qkv, n_seq),), seq_layout, halve_order, "seq", n_seq, seq_index, add_parts
    )
    own_qkv = own_qkv.astype(jnp.bfloat16)
    query = ag_doubling(own_qkv[:, :feat_width], "seq", n_seq, double_order, seq_index)
    key_new = own_qkv[:, feat_width : 2 * feat_width]
    val_new = own_qkv[:, 2 * feat_width :]
    head_first = (tp_index * local_heads).astype(jnp.float32)
    slopes = jnp.exp2(
        -8.0 * (head_first + jnp.arange(local_heads, dtype=jnp.float32) + 1.0) / HEADS
    )
    placed, inverse = stable_ranks(group_ids)
    members = placed.reshape(groups, requests // groups)
    group_match = group_ids[:, None] == jnp.arange(groups, dtype=jnp.int32)[None, :]
    req_prompt = jnp.sum(jnp.where(group_match, prompt_len[None, :], 0), 1)
    query_pos = (req_prompt + cont_len)[:, None] + jnp.arange(NEW, dtype=jnp.int32)[None, :]
    query_req = query.reshape(requests, NEW, local_heads, HD)
    group_query = query_req[members].reshape(groups, -1, local_heads, HD)
    group_pos = query_pos[members].reshape(groups, -1)
    key_slab = prompt_key.reshape(groups, block_len, local_heads, HD)
    val_slab = prompt_val.reshape(groups, block_len, local_heads, HD)
    key_pos = seq_index * block_len + jnp.arange(block_len, dtype=jnp.int32)
    scores = jnp.einsum(
        "gqhd,gphd->ghqp", group_query, key_slab, preferred_element_type=jnp.float32
    )
    distance = (key_pos[None, None, :] - group_pos[:, :, None]).astype(jnp.float32)
    scores = scores * score_scale + slopes[None, :, None, None] * distance[:, None, :, :]
    is_live = (key_pos[None, :] < prompt_len[:, None])[:, None, None, :]
    block_top = jnp.max(jnp.where(is_live, scores, NEG_FILL), -1)
    weights = jnp.where(is_live, jnp.exp(scores - block_top[..., None]), 0.0)
    block_sum = jnp.sum(weights, -1)
    block_acc = jnp.einsum(
        "ghqp,gphd->gqhd",
        weights.astype(jnp.bfloat16),
        val_slab,
        preferred_element_type=jnp.float32,
    )
    prompt_top = (
        jnp.transpose(block_top, (0, 2, 1))
        .reshape(requests, NEW, local_heads)[inverse]
        .reshape(row_count, local_heads)
    )
    prompt_sum = (
        jnp.transpose(block_sum, (0, 2, 1))
        .reshape(requests, NEW, local_heads)[inverse]
        .reshape(row_count, local_heads)
    )
    prompt_acc = block_acc.reshape(requests, NEW, local_heads, HD)[inverse].reshape(
        row_count, local_heads, HD
    )
    home_query = own_qkv[:, :feat_width].reshape(home_requests, NEW, local_heads, HD)
    home_pos = lax.dynamic_slice_in_dim(query_pos, seq_index * home_requests, home_requests, 0)
    home_prompt = lax.dynamic_slice_in_dim(req_prompt, seq_index * home_requests, home_requests, 0)
    home_filled = lax.dynamic_slice_in_dim(cont_len, seq_index * home_requests, home_requests, 0)
    cache_keys = cont_key.reshape(home_requests, slots, local_heads, HD)
    cache_vals = cont_val.reshape(home_requests, slots, local_heads, HD)
    slot_index = jnp.arange(slots, dtype=jnp.int32)
    cache_pos = home_prompt[:, None] + slot_index[None, :]
    cache_scores = (
        jnp.einsum("rjhd,rkhd->rhjk", home_query, cache_keys, preferred_element_type=jnp.float32)
        * score_scale
    )
    cache_scores = cache_scores + slopes[None, :, None, None] * (
        cache_pos[:, None, None, :] - home_pos[:, None, :, None]
    ).astype(jnp.float32)
    cache_live = (slot_index[None, :] < home_filled[:, None])[:, None, None, :]
    fresh_keys = key_new.reshape(home_requests, NEW, local_heads, HD)
    fresh_vals = val_new.reshape(home_requests, NEW, local_heads, HD)
    steps_new = jnp.arange(NEW, dtype=jnp.int32)
    fresh_dist = (steps_new[None, :] - steps_new[:, None]).astype(jnp.float32)
    fresh_scores = (
        jnp.einsum("rjhd,rkhd->rhjk", home_query, fresh_keys, preferred_element_type=jnp.float32)
        * score_scale
    )
    fresh_scores = fresh_scores + slopes[None, :, None, None] * fresh_dist[None, None, :, :]
    fresh_live = (steps_new[None, :] <= steps_new[:, None])[None, None, :, :]
    home_top = jnp.maximum(
        jnp.max(jnp.where(cache_live, cache_scores, NEG_FILL), -1),
        jnp.max(jnp.where(fresh_live, fresh_scores, NEG_FILL), -1),
    )
    cache_weights = jnp.where(cache_live, jnp.exp(cache_scores - home_top[..., None]), 0.0)
    fresh_weights = jnp.where(fresh_live, jnp.exp(fresh_scores - home_top[..., None]), 0.0)
    home_sum = jnp.sum(cache_weights, -1) + jnp.sum(fresh_weights, -1)
    home_acc = jnp.einsum(
        "rhjk,rkhd->rjhd",
        cache_weights.astype(jnp.bfloat16),
        cache_vals,
        preferred_element_type=jnp.float32,
    )
    home_acc = home_acc + jnp.einsum(
        "rhjk,rkhd->rjhd",
        fresh_weights.astype(jnp.bfloat16),
        fresh_vals,
        preferred_element_type=jnp.float32,
    )
    home_top = jnp.transpose(home_top, (0, 2, 1)).reshape(home_rows, local_heads)
    home_sum = jnp.transpose(home_sum, (0, 2, 1)).reshape(home_rows, local_heads)
    home_acc = home_acc.reshape(home_rows, local_heads, HD)
    merge = packed_merge(feat_width, local_heads)
    packed = jnp.concatenate(
        [prompt_acc.reshape(row_count, feat_width), prompt_top, prompt_sum], -1
    )
    home_packed = jnp.concatenate([home_acc.reshape(home_rows, feat_width), home_top, home_sum], -1)
    row_start = seq_index * home_rows
    (own_rows,) = merge((lax.dynamic_slice_in_dim(packed, row_start, home_rows, 0),), (home_packed,))
    packed = lax.dynamic_update_slice_in_dim(packed, own_rows, row_start, 0)
    near_bits = halve_order[:2]
    far_bits = halve_order[2:]
    (packed,) = rs_two_link(
        (to_blocks(packed, n_seq),), seq_layout, near_bits, "seq", n_seq, seq_index, merge
    )
    for bit in far_bits:
        (packed,) = merge((packed,), (lax.ppermute(packed, "seq", _pairs(n_seq, bit)),))
    part_attended = (
        packed[..., :feat_width].reshape(packed.shape[:-1] + (local_heads, HD))
        / packed[..., feat_width + local_heads :][..., None]
    ).reshape(packed.shape[:-1] + (feat_width,)).astype(jnp.bfloat16)
    near_have = [b for b in seq_layout if b not in near_bits]
    attended, _ = ag_place(
        part_attended, near_have, near_bits[::-1], seq_layout, "seq", n_seq, seq_index
    )
    attended = attended.reshape(row_count, feat_width)
    attn_sum = ar_doubling(
        jnp.dot(attended, w_out, preferred_element_type=jnp.float32), "tp", n_tp, tp_bits
    )
    hidden_state = token_float + attn_sum
    second_stats = ar_doubling(
        jnp.stack([jnp.sum(hidden_state, 1), jnp.sum(hidden_state * hidden_state, 1)]),
        "seq", n_seq, halve_order,
    )
    second_normed = finish_norm(hidden_state, second_stats[0], second_stats[1], ln_second_gain)
    halves = w_up.shape[1] // 2
    up_part = jnp.einsum(
        "rk,kcn->crn",
        second_normed,
        w_up.reshape(w_up.shape[0], 2, halves),
        preferred_element_type=jnp.float32,
    )
    own_up = rs_tiled(up_part, "seq", n_seq, halve_order, seq_index)
    own_activated = jax.nn.gelu(own_up, approximate=False).astype(jnp.bfloat16)
    activated = ag_tiled(own_activated, "seq", n_seq, double_order, seq_index, row_count, halves)
    down_part = jnp.einsum(
        "crn,cnf->rf",
        activated,
        w_down.reshape(2, halves, w_down.shape[1]),
        preferred_element_type=jnp.float32,
    )
    down_sum = down_part
    for bit in tp_bits:
        sent = down_sum.astype(jnp.bfloat16)
        down_sum = sent.astype(jnp.float32) + lax.ppermute(sent, "tp", _pairs(n_tp, bit)).astype(
            jnp.float32
        )
    return (hidden_state + down_sum).astype(jnp.bfloat16)


def solution(mesh):
    in_specs = (
        P(None, "seq"),
        P("seq"),
        P("seq", None, "tp"),
        P("tp", "seq"),
        P("seq"),
        P("seq", "tp"),
        P("tp", "seq"),
        P(None, "seq", "tp"),
        P(None, "seq", "tp"),
        P("seq", None, "tp"),
        P("seq", None, "tp"),
        P(),
        P(),
        P(),
    )
    out_specs = P(None, "seq")
    return jax.shard_map(body, mesh=mesh, in_specs=in_specs, out_specs=out_specs, check_vma=False)
```

```python
import math

import jax
import jax.numpy as jnp
from jax import lax
from jax.sharding import PartitionSpec as P

D = 4096
HEADS = 32
HD = 128
NEW = 4


NEG_FILL = -1e30
NORM_EPS = 1e-05


def finish_norm(values, row_sum, row_square, gain):
    mean_row = row_sum / D
    variance = row_square / D - mean_row * mean_row
    scaled = (values - mean_row[:, None]) * lax.rsqrt(variance + NORM_EPS)[:, None]
    return (scaled * gain.astype(jnp.float32)[None, :]).astype(jnp.bfloat16)


def combine_parts(earlier, later):
    merged_top = jnp.maximum(earlier[0], later[0])
    left_factor = jnp.exp(earlier[0] - merged_top)
    right_factor = jnp.exp(later[0] - merged_top)
    merged_sum = earlier[1] * left_factor + later[1] * right_factor
    merged_acc = earlier[2] * left_factor[..., None] + later[2] * right_factor[..., None]
    return (merged_top, merged_sum, merged_acc)


def _levels(n):
    return n.bit_length() - 1


def _pairs(n, bit):
    return [(i, i ^ (1 << bit)) for i in range(n)]


def ar_doubling(x, axis, n, order):
    for bit in order:
        x = x + lax.ppermute(x, axis, _pairs(n, bit))
    return x


def add_parts(keep, got):
    return tuple(a + b for a, b in zip(keep, got))


def to_blocks(p, n):
    return p.reshape((2,) * _levels(n) + (p.shape[0] // n,) + p.shape[1:])


def rs_steps(parts, remaining, bits, axis, n, index, merge):
    remaining = list(remaining)
    for bit in bits:
        ax = remaining.index(bit)
        mine = (index >> bit) & 1
        keep = tuple(lax.dynamic_index_in_dim(p, mine, ax, keepdims=False) for p in parts)
        send = tuple(lax.dynamic_index_in_dim(p, 1 - mine, ax, keepdims=False) for p in parts)
        got = lax.ppermute(send, axis, _pairs(n, bit))
        parts = merge(keep, got)
        remaining.remove(bit)
    return parts, remaining


def rs_sum(x, axis, n, order, index, split):
    remaining = list(range(_levels(n) - 1, -1, -1))
    blocks = to_blocks(x, n)
    if split:
        half = x.shape[-1] // 2
        (low,), after = rs_steps((blocks[..., :half],), remaining, order[:2], axis, n, index, add_parts)
        (high,), _ = rs_steps((blocks[..., half:],), remaining, order[1::-1], axis, n, index, add_parts)
        blocks = jnp.concatenate([low, high], -1)
        remaining, order = after, order[2:]
    (out,), _ = rs_steps((blocks,), remaining, order, axis, n, index, add_parts)
    return out


def ag_steps(x, have, bits, axis, n, index):
    have = list(have)
    for bit in bits:
        got = lax.ppermute(x, axis, _pairs(n, bit))
        first = ((index >> bit) & 1) == 0
        low = jnp.where(first, x, got)
        high = jnp.where(first, got, x)
        pos = sum(1 for b in have if b > bit)
        x = jnp.stack([low, high], axis=pos)
        have.insert(pos, bit)
    return x, have


def ag_doubling(x, axis, n, order, index, split=False):
    levels = _levels(n)
    if split:
        x, have = ag_steps(x, [], order[:-2], axis, n, index)
        half = x.shape[-1] // 2
        low, _ = ag_steps(x[..., :half], have, order[-2:], axis, n, index)
        high, _ = ag_steps(x[..., half:], have, order[-2:][::-1], axis, n, index)
        x = jnp.concatenate([low, high], -1)
    else:
        x, _ = ag_steps(x, [], order, axis, n, index)
    return x.reshape((-1,) + x.shape[levels + 1 :])


def tiled_layout(n, rows, cols):
    levels = _levels(n)
    row_bits = levels - 1
    shape = (2,) + (2,) * row_bits + (rows >> row_bits, cols)
    layout = [0] + list(range(levels - 1, 0, -1)) + ["r", "c"]
    return shape, layout


def rs_tiled(x, axis, n, order, index):
    shape, layout = tiled_layout(n, x.shape[1], x.shape[2])
    blocks = x.reshape(shape)
    top_bit = _levels(n) - 1
    cut = layout.index(top_bit)
    low = lax.slice_in_dim(blocks, 0, 1, axis=cut)
    high = lax.slice_in_dim(blocks, 1, 2, axis=cut)
    (low,), after = rs_steps((low,), layout, order[:2], axis, n, index, add_parts)
    (high,), _ = rs_steps((high,), layout, order[1::-1], axis, n, index, add_parts)
    joined = jnp.concatenate([low, high], after.index(top_bit))
    (out,), _ = rs_steps((joined,), after, order[2:], axis, n, index, add_parts)
    return out


def ag_place(x, have, bits, layout, axis, n, index):
    have = list(have)
    for bit in bits:
        got = lax.ppermute(x, axis, _pairs(n, bit))
        first = ((index >> bit) & 1) == 0
        low = jnp.where(first, x, got)
        high = jnp.where(first, got, x)
        rank = layout.index(bit)
        pos = sum(1 for b in have if layout.index(b) < rank)
        x = jnp.stack([low, high], axis=pos)
        have.insert(pos, bit)
    return x, have


def ag_tiled(x, axis, n, order, index, rows, cols):
    shape, layout = tiled_layout(n, rows, cols)
    top_bit = _levels(n) - 1
    x, have = ag_place(x, ["r", "c"], order[:-2], layout, axis, n, index)
    cut = have.index(top_bit)
    low, done = ag_place(
        lax.slice_in_dim(x, 0, 1, axis=cut), have, order[-2:], layout, axis, n, index
    )
    high, _ = ag_place(
        lax.slice_in_dim(x, 1, 2, axis=cut), have, order[-2:][::-1], layout, axis, n, index
    )
    joined = jnp.concatenate([low, high], done.index(top_bit))
    return joined.reshape(2, rows, cols)


def rs_two_link(blocks, layout, order, axis, n, index, merge):
    top_bit = _levels(n) - 1
    cut = layout.index(top_bit)
    low = tuple(lax.slice_in_dim(p, 0, 1, axis=cut) for p in blocks)
    high = tuple(lax.slice_in_dim(p, 1, 2, axis=cut) for p in blocks)
    low, after = rs_steps(low, layout, order[:2], axis, n, index, merge)
    high, _ = rs_steps(high, layout, order[1::-1], axis, n, index, merge)
    at = after.index(top_bit)
    joined = tuple(jnp.concatenate([a, b], at) for a, b in zip(low, high))
    out, _ = rs_steps(joined, after, order[2:], axis, n, index, merge)
    return out


def stable_ranks(keys):
    count = keys.shape[0]
    order = jnp.arange(count, dtype=jnp.int32)
    before = (keys[None, :] < keys[:, None]) | (
        (keys[None, :] == keys[:, None]) & (order[None, :] < order[:, None])
    )
    rank = jnp.sum(before.astype(jnp.int32), 1)
    placed = jnp.sum(jnp.where(rank[None, :] == order[:, None], order[None, :], 0), 1)
    return placed, rank


def packed_merge(width, heads):
    def merge(keep, got):
        (mine,), (other,) = keep, got
        top = jnp.maximum(mine[..., width : width + heads], other[..., width : width + heads])
        mine_f = jnp.exp(mine[..., width : width + heads] - top)
        other_f = jnp.exp(other[..., width : width + heads] - top)
        total = mine[..., width + heads :] * mine_f + other[..., width + heads :] * other_f
        shape = mine.shape[:-1] + (heads, width // heads)
        acc = (
            mine[..., :width].reshape(shape) * mine_f[..., None]
            + other[..., :width].reshape(shape) * other_f[..., None]
        ).reshape(mine.shape[:-1] + (width,))
        return (jnp.concatenate([acc, top, total], -1),)

    return merge


def seq_orders(n):
    levels = _levels(n)
    near = [b for b in (0, 2, 1, 3, 4) if b < levels] + list(range(5, levels))
    return near, near[::-1]


def tp_order(n):
    return list(range(_levels(n)))


def body(
    tokens,
    ln_first_gain,
    w_qkv,
    w_out,
    ln_second_gain,
    w_up,
    w_down,
    prompt_key,
    prompt_val,
    cont_key,
    cont_val,
    group_ids,
    prompt_len,
    cont_len,
):
    row_count = tokens.shape[0]
    seq_index = lax.axis_index("seq")
    tp_index = lax.axis_index("tp")
    n_seq = lax.axis_size("seq")
    n_tp = lax.axis_size("tp")
    halve_order, double_order = seq_orders(n_seq)
    tp_bits = tp_order(n_tp)
    feat_width = w_qkv.shape[2]
    local_heads = feat_width // HD
    home_requests = cont_key.shape[0]
    home_rows = home_requests * NEW
    requests = row_count // NEW
    groups = prompt_key.shape[0]
    block_len = prompt_key.shape[1]
    slots = cont_key.shape[1]
    score_scale = 1.0 / math.sqrt(HD)
    token_float = tokens.astype(jnp.float32)
    first_stats = ar_doubling(
        jnp.stack([jnp.sum(token_float, 1), jnp.sum(token_float * token_float, 1)]),
        "seq", n_seq, halve_order,
    )
    normed = finish_norm(token_float, first_stats[0], first_stats[1], ln_first_gain)
    w_flat = w_qkv.reshape(w_qkv.shape[0], 3 * feat_width)
    partial_qkv = jnp.dot(normed, w_flat, preferred_element_type=jnp.float32)
    seq_layout = list(range(_levels(n_seq) - 1, -1, -1)) + ["r", "c"]
    (own_qkv,) = rs_two_link(
        (to_blocks(partial_qkv, n_seq),), seq_layout, halve_order, "seq", n_seq, seq_index, add_parts
    )
    own_qkv = own_qkv.astype(jnp.bfloat16)
    query = ag_doubling(own_qkv[:, :feat_width], "seq", n_seq, double_order, seq_index, True)
    key_new = own_qkv[:, feat_width : 2 * feat_width]
    val_new = own_qkv[:, 2 * feat_width :]
    head_first = (tp_index * local_heads).astype(jnp.float32)
    slopes = jnp.exp2(
        -8.0 * (head_first + jnp.arange(local_heads, dtype=jnp.float32) + 1.0) / HEADS
    )
    placed, inverse = stable_ranks(group_ids)
    members = placed.reshape(groups, requests // groups)
    group_match = group_ids[:, None] == jnp.arange(groups, dtype=jnp.int32)[None, :]
    req_prompt = jnp.sum(jnp.where(group_match, prompt_len[None, :], 0), 1)
    query_pos = (req_prompt + cont_len)[:, None] + jnp.arange(NEW, dtype=jnp.int32)[None, :]
    query_req = query.reshape(requests, NEW, local_heads, HD)
    group_query = query_req[members].reshape(groups, -1, local_heads, HD)
    group_pos = query_pos[members].reshape(groups, -1)
    key_slab = prompt_key.reshape(groups, block_len, local_heads, HD)
    val_slab = prompt_val.reshape(groups, block_len, local_heads, HD)
    key_pos = seq_index * block_len + jnp.arange(block_len, dtype=jnp.int32)
    scores = jnp.einsum(
        "gqhd,gphd->ghqp", group_query, key_slab, preferred_element_type=jnp.float32
    )
    distance = (key_pos[None, None, :] - group_pos[:, :, None]).astype(jnp.float32)
    scores = scores * score_scale + slopes[None, :, None, None] * distance[:, None, :, :]
    is_live = (key_pos[None, :] < prompt_len[:, None])[:, None, None, :]
    block_top = jnp.max(jnp.where(is_live, scores, NEG_FILL), -1)
    weights = jnp.where(is_live, jnp.exp(scores - block_top[..., None]), 0.0)
    block_sum = jnp.sum(weights, -1)
    block_acc = jnp.einsum(
        "ghqp,gphd->gqhd",
        weights.astype(jnp.bfloat16),
        val_slab,
        preferred_element_type=jnp.float32,
    )
    prompt_top = (
        jnp.transpose(block_top, (0, 2, 1))
        .reshape(requests, NEW, local_heads)[inverse]
        .reshape(row_count, local_heads)
    )
    prompt_sum = (
        jnp.transpose(block_sum, (0, 2, 1))
        .reshape(requests, NEW, local_heads)[inverse]
        .reshape(row_count, local_heads)
    )
    prompt_acc = block_acc.reshape(requests, NEW, local_heads, HD)[inverse].reshape(
        row_count, local_heads, HD
    )
    home_query = own_qkv[:, :feat_width].reshape(home_requests, NEW, local_heads, HD)
    home_pos = lax.dynamic_slice_in_dim(query_pos, seq_index * home_requests, home_requests, 0)
    home_prompt = lax.dynamic_slice_in_dim(req_prompt, seq_index * home_requests, home_requests, 0)
    home_filled = lax.dynamic_slice_in_dim(cont_len, seq_index * home_requests, home_requests, 0)
    cache_keys = cont_key.reshape(home_requests, slots, local_heads, HD)
    cache_vals = cont_val.reshape(home_requests, slots, local_heads, HD)
    slot_index = jnp.arange(slots, dtype=jnp.int32)
    cache_pos = home_prompt[:, None] + slot_index[None, :]
    cache_scores = (
        jnp.einsum("rjhd,rkhd->rhjk", home_query, cache_keys, preferred_element_type=jnp.float32)
        * score_scale
    )
    cache_scores = cache_scores + slopes[None, :, None, None] * (
        cache_pos[:, None, None, :] - home_pos[:, None, :, None]
    ).astype(jnp.float32)
    cache_live = (slot_index[None, :] < home_filled[:, None])[:, None, None, :]
    fresh_keys = key_new.reshape(home_requests, NEW, local_heads, HD)
    fresh_vals = val_new.reshape(home_requests, NEW, local_heads, HD)
    steps_new = jnp.arange(NEW, dtype=jnp.int32)
    fresh_dist = (steps_new[None, :] - steps_new[:, None]).astype(jnp.float32)
    fresh_scores = (
        jnp.einsum("rjhd,rkhd->rhjk", home_query, fresh_keys, preferred_element_type=jnp.float32)
        * score_scale
    )
    fresh_scores = fresh_scores + slopes[None, :, None, None] * fresh_dist[None, None, :, :]
    fresh_live = (steps_new[None, :] <= steps_new[:, None])[None, None, :, :]
    home_top = jnp.maximum(
        jnp.max(jnp.where(cache_live, cache_scores, NEG_FILL), -1),
        jnp.max(jnp.where(fresh_live, fresh_scores, NEG_FILL), -1),
    )
    cache_weights = jnp.where(cache_live, jnp.exp(cache_scores - home_top[..., None]), 0.0)
    fresh_weights = jnp.where(fresh_live, jnp.exp(fresh_scores - home_top[..., None]), 0.0)
    home_sum = jnp.sum(cache_weights, -1) + jnp.sum(fresh_weights, -1)
    home_acc = jnp.einsum(
        "rhjk,rkhd->rjhd",
        cache_weights.astype(jnp.bfloat16),
        cache_vals,
        preferred_element_type=jnp.float32,
    )
    home_acc = home_acc + jnp.einsum(
        "rhjk,rkhd->rjhd",
        fresh_weights.astype(jnp.bfloat16),
        fresh_vals,
        preferred_element_type=jnp.float32,
    )
    home_top = jnp.transpose(home_top, (0, 2, 1)).reshape(home_rows, local_heads)
    home_sum = jnp.transpose(home_sum, (0, 2, 1)).reshape(home_rows, local_heads)
    home_acc = home_acc.reshape(home_rows, local_heads, HD)
    merge = packed_merge(feat_width, local_heads)
    packed = jnp.concatenate(
        [prompt_acc.reshape(row_count, feat_width), prompt_top, prompt_sum], -1
    )
    home_packed = jnp.concatenate([home_acc.reshape(home_rows, feat_width), home_top, home_sum], -1)
    row_start = seq_index * home_rows
    (own_rows,) = merge((lax.dynamic_slice_in_dim(packed, row_start, home_rows, 0),), (home_packed,))
    packed = lax.dynamic_update_slice_in_dim(packed, own_rows, row_start, 0)
    near_bits = halve_order[:2]
    far_bits = halve_order[2:]
    (packed,) = rs_two_link(
        (to_blocks(packed, n_seq),), seq_layout, near_bits, "seq", n_seq, seq_index, merge
    )
    for bit in far_bits:
        (packed,) = merge((packed,), (lax.ppermute(packed, "seq", _pairs(n_seq, bit)),))
    part_attended = (
        packed[..., :feat_width].reshape(packed.shape[:-1] + (local_heads, HD))
        / packed[..., feat_width + local_heads :][..., None]
    ).reshape(packed.shape[:-1] + (feat_width,)).astype(jnp.bfloat16)
    near_have = [b for b in seq_layout if b not in near_bits]
    attended, _ = ag_place(
        part_attended, near_have, near_bits[::-1], seq_layout, "seq", n_seq, seq_index
    )
    attended = attended.reshape(row_count, feat_width)
    attn_sum = ar_doubling(
        jnp.dot(attended, w_out, preferred_element_type=jnp.float32), "tp", n_tp, tp_bits
    )
    hidden_state = token_float + attn_sum
    second_stats = ar_doubling(
        jnp.stack([jnp.sum(hidden_state, 1), jnp.sum(hidden_state * hidden_state, 1)]),
        "seq", n_seq, halve_order,
    )
    second_normed = finish_norm(hidden_state, second_stats[0], second_stats[1], ln_second_gain)
    halves = w_up.shape[1] // 2
    up_part = jnp.einsum(
        "rk,kcn->crn",
        second_normed,
        w_up.reshape(w_up.shape[0], 2, halves),
        preferred_element_type=jnp.float32,
    )
    own_up = rs_tiled(up_part, "seq", n_seq, halve_order, seq_index)
    own_activated = jax.nn.gelu(own_up, approximate=False).astype(jnp.bfloat16)
    activated = ag_tiled(own_activated, "seq", n_seq, double_order, seq_index, row_count, halves)
    down_part = jnp.einsum(
        "crn,cnf->rf",
        activated,
        w_down.reshape(2, halves, w_down.shape[1]),
        preferred_element_type=jnp.float32,
    )
    down_sum = down_part
    for bit in tp_bits:
        sent = down_sum.astype(jnp.bfloat16)
        down_sum = sent.astype(jnp.float32) + lax.ppermute(sent, "tp", _pairs(n_tp, bit)).astype(
            jnp.float32
        )
    return (hidden_state + down_sum).astype(jnp.bfloat16)


def solution(mesh):
    in_specs = (
        P(None, "seq"),
        P("seq"),
        P("seq", None, "tp"),
        P("tp", "seq"),
        P("seq"),
        P("seq", "tp"),
        P("tp", "seq"),
        P(None, "seq", "tp"),
        P(None, "seq", "tp"),
        P("seq", None, "tp"),
        P("seq", None, "tp"),
        P(),
        P(),
        P(),
    )
    out_specs = P(None, "seq")
    return jax.shard_map(body, mesh=mesh, in_specs=in_specs, out_specs=out_specs, check_vma=False)
```
